256 devices in a mesh: dp: 16 (over x, y_hi, core), seq: 16 (over z, y_lo).
Axes of the slice: x: 4, y: 4 (y_hi: 2, y_lo: 2; y = y_hi * 2 + y_lo), z: 8, core: 2. Of those that a mesh axis runs over, the one named last changes fastest.
Arguments:
- queries: bfloat16 [40960, 768], P(('dp', 'seq')), may hold values from -8 to 8
- keys: bfloat16 [40960, 768], P(('dp', 'seq')), may hold values from -8 to 8
- values: bfloat16 [40960, 768], P(('dp', 'seq')), may hold values from -6 to 6
- frames: bfloat16 [40960, 768], P(('dp', 'seq')), may hold values from -4 to 4
- upstream: bfloat16 [40960, 768], P(('dp', 'seq')), may hold values from -6 to 6
- lengths: int32 [16], P('dp'), may hold values from 640 to 2560, as said below
- conv_kernel: bfloat16 [32, 768], replicated, may hold values from -1 to 1
Outputs:
- out: bfloat16 [40960, 768], P(('dp', 'seq'))
- query_grad: bfloat16 [40960, 768], P(('dp', 'seq'))
- key_grad: bfloat16 [40960, 768], P(('dp', 'seq'))
- value_grad: bfloat16 [40960, 768], P(('dp', 'seq'))
- frame_grad: bfloat16 [40960, 768], P(('dp', 'seq'))
- kernel_grad: float32 [32, 768], replicated
The draws below stay inside these ranges and needn't reach their ends.
Inputs may be any that keep to these rules, and one draw needn't show every extreme that they name: `lengths`: one utterance has all 2560 frames live and another has 640.
All inputs are finite; a program needn't handle non-finite values.
Results may differ from the reference program's by a relative error of at most 0.0262.
Values may be sent and summed in bfloat16 or wider, within the bound.
No kernel may reach another device: no remote copies, remote signals or barrier semaphores. Data moves between devices by JAX's collectives and lax.ppermute only.
A program may use at most 128 MiB of HBM per device.

```python
import jax
import jax.numpy as jnp
from jax import lax

HEADS = 12
HEAD_DIM = 64
CHANNELS = 768
KERNEL = 32
UTTS = 16
SEQLEN = 2560
TOKENS = 40960


def paired_rows(key):
    base_key = jax.random.fold_in(key, 7001)
    query_key = jax.random.fold_in(base_key, 1)
    key_key = jax.random.fold_in(base_key, 2)
    query_rows = jnp.clip(1.5 * jax.random.normal(query_key, (TOKENS, CHANNELS), jnp.float32), -6.0, 6.0)
    key_rows = jnp.clip(1.5 * jax.random.normal(key_key, (TOKENS, CHANNELS), jnp.float32), -6.0, 6.0)
    return (query_rows, key_rows)


def draw_queries(key, part):
    return paired_rows(key)[0].astype(jnp.bfloat16)


def draw_keys(key, part):
    return paired_rows(key)[1].astype(jnp.bfloat16)


def draw_lengths(key, part):
    length_key = jax.random.fold_in(key, 9001)
    drawn = jax.random.randint(jax.random.fold_in(length_key, 1), (UTTS,), SEQLEN // 4, SEQLEN + 1)
    order = jax.random.permutation(jax.random.fold_in(length_key, 2), UTTS)
    drawn = drawn.at[order[0]].set(SEQLEN)
    drawn = drawn.at[order[1]].set(SEQLEN // 4)
    return drawn.astype(jnp.int32)


def level_of(rng, dims, pieces, low, top_value):
    def one(axis_at, blocks):
        steps = jax.random.uniform(jax.random.fold_in(jax.random.fold_in(rng, 6), axis_at), (blocks,), jnp.float32, low / len(pieces), top_value / len(pieces))
        return jnp.repeat(jnp.exp(steps), dims[axis_at] // blocks).reshape((-1,) + (1,) * (len(dims) - axis_at - 1))

    factor_of = one(*pieces[0])
    for cut in pieces[1:]:
        factor_of = factor_of * one(*cut)
    return factor_of


def centred(stream_key, dims, deviation, most, cuts=(), kind=jnp.bfloat16):
    factor_of = level_of(stream_key, dims, cuts, -0.22, 0.18) if cuts else 1.0
    values = jax.random.normal(stream_key, dims, jnp.float32) * deviation * factor_of
    return jnp.minimum(jnp.maximum(values, -most), most).astype(kind)


def setup_inputs(seed: int = 0) -> dict:
    seeds = jax.random.split(jax.random.key(seed), 8)
    queries = draw_queries(jax.random.fold_in(seeds[7], 71), 0)
    keys = draw_keys(jax.random.fold_in(seeds[7], 71), 0)
    values = centred(seeds[2], (TOKENS, CHANNELS), 1.0, 6.0, ((0, 256),))
    frames = centred(seeds[3], (TOKENS, CHANNELS), 0.5, 4.0, ((0, 256),))
    upstream = centred(seeds[4], (TOKENS, CHANNELS), 1.0, 6.0, ((0, 256),))
    lengths = draw_lengths(jax.random.fold_in(seeds[7], 71), 0)
    conv_kernel = centred(seeds[6], (KERNEL, CHANNELS), KERNEL ** -0.5, 1.0)
    return {"queries": queries, "keys": keys, "values": values, "frames": frames, "upstream": upstream, "lengths": lengths, "conv_kernel": conv_kernel}


def split_heads(flat_array):
    return flat_array.reshape(SEQLEN, HEADS, HEAD_DIM).transpose(1, 0, 2)


def merge_heads(head_array):
    return head_array.transpose(1, 0, 2).reshape(SEQLEN, CHANNELS)


def utterance_pass(queries, keys, values, frames, upstream, length, weights):
    score_scale = HEAD_DIM ** -0.5
    positions = jnp.arange(SEQLEN, dtype=jnp.int32)
    key_live = positions < length
    frame_live = key_live[:, None]

    def head_scores(query_head, key_head):
        scores = jnp.dot(query_head, key_head.T, preferred_element_type=jnp.float32) * score_scale
        return jnp.where(key_live[None, :], scores, -jnp.inf)

    def forward_head(head_items):
        query_head, key_head, value_head = head_items
        scores = head_scores(query_head, key_head)
        running_top = jnp.max(scores, axis=1)
        log_total = running_top + jnp.log(jnp.sum(jnp.exp(scores - running_top[:, None]), axis=1))
        prob_bf = jnp.exp(scores - log_total[:, None]).astype(jnp.bfloat16)
        attended_head = jnp.dot(prob_bf, value_head, preferred_element_type=jnp.float32).astype(jnp.bfloat16)
        return attended_head, log_total

    query_heads = split_heads(queries)
    key_heads = split_heads(keys)
    value_heads = split_heads(values)
    attended_heads, log_totals = lax.map(forward_head, (query_heads, key_heads, value_heads))
    attended = merge_heads(attended_heads)
    hidden = (frames.astype(jnp.float32) + attended.astype(jnp.float32)).astype(jnp.bfloat16)
    masked = jnp.where(frame_live, hidden, jnp.zeros_like(hidden)).astype(jnp.float32)
    padded = jnp.concatenate([jnp.zeros((KERNEL - 1, CHANNELS), jnp.float32), masked], axis=0)
    conv_out = jnp.zeros((SEQLEN, CHANNELS), jnp.float32)
    for tap_index in range(KERNEL):
        conv_out = conv_out + weights[tap_index] * padded[KERNEL - 1 - tap_index:KERNEL - 1 - tap_index + SEQLEN]
    sig_conv = jax.nn.sigmoid(conv_out)
    out = (hidden.astype(jnp.float32) + conv_out * sig_conv).astype(jnp.bfloat16)
    loss_grad = jnp.where(frame_live, upstream.astype(jnp.float32), 0.0)
    conv_rounded = (loss_grad * sig_conv * (1.0 + conv_out * (1.0 - sig_conv))).astype(jnp.bfloat16)
    conv_grad = lax.optimization_barrier(conv_rounded).astype(jnp.float32)
    kernel_terms = jnp.stack([jnp.sum(conv_grad * padded[KERNEL - 1 - tap_index:KERNEL - 1 - tap_index + SEQLEN], axis=0) for tap_index in range(KERNEL)])
    ahead_rows = jnp.concatenate([conv_grad, jnp.zeros((KERNEL - 1, CHANNELS), jnp.float32)], axis=0)
    back_conv = jnp.zeros((SEQLEN, CHANNELS), jnp.float32)
    for tap_index in range(KERNEL):
        back_conv = back_conv + weights[tap_index] * ahead_rows[tap_index:tap_index + SEQLEN]
    frame_grad = (loss_grad + jnp.where(frame_live, back_conv, 0.0)).astype(jnp.bfloat16)
    grad_heads = split_heads(frame_grad)
    delta_rows = jnp.sum(grad_heads.astype(jnp.float32) * attended_heads.astype(jnp.float32), axis=2)

    def backward_head(head_items):
        query_head, key_head, value_head, grad_head, log_total, delta_head = head_items
        scores = head_scores(query_head, key_head)
        soft_weights = jnp.exp(scores - log_total[:, None])
        prob_bf = soft_weights.astype(jnp.bfloat16)
        prob_grad = jnp.dot(grad_head, value_head.T, preferred_element_type=jnp.float32)
        score_grad = (soft_weights * (prob_grad - delta_head[:, None])).astype(jnp.bfloat16)
        query_part = (jnp.dot(score_grad, key_head, preferred_element_type=jnp.float32) * score_scale).astype(jnp.bfloat16)
        key_part = (jnp.dot(score_grad.T, query_head, preferred_element_type=jnp.float32) * score_scale).astype(jnp.bfloat16)
        value_part = jnp.dot(prob_bf.T, grad_head, preferred_element_type=jnp.float32).astype(jnp.bfloat16)
        return query_part, key_part, value_part

    query_grads, key_grads, value_grads = lax.map(backward_head, (query_heads, key_heads, value_heads, grad_heads, log_totals, delta_rows))
    return out, merge_heads(query_grads), merge_heads(key_grads), merge_heads(value_grads), frame_grad, kernel_terms


def reference(queries, keys, values, frames, upstream, lengths, conv_kernel):
    weights = conv_kernel.astype(jnp.float32)
    stacked_shape = (UTTS, SEQLEN, CHANNELS)

    def per_utterance(utt_items):
        return utterance_pass(utt_items[0], utt_items[1], utt_items[2], utt_items[3], utt_items[4], utt_items[5], weights)

    results = lax.map(per_utterance, (queries.reshape(stacked_shape), keys.reshape(stacked_shape), values.reshape(stacked_shape), frames.reshape(stacked_shape), upstream.reshape(stacked_shape), lengths))
    out, query_grad, key_grad, value_grad, frame_grad, kernel_terms = results
    kernel_grad = jnp.sum(kernel_terms, axis=0) / UTTS
    full_shape = (TOKENS, CHANNELS)
    return (out.reshape(full_shape), query_grad.reshape(full_shape), key_grad.reshape(full_shape), value_grad.reshape(full_shape), frame_grad.reshape(full_shape), kernel_grad)
```

```python
import jax
import jax.numpy as jnp
from jax import lax
from jax.sharding import Mesh
from jax.sharding import PartitionSpec as P

HEAD_DIM = 64
KERNEL = 32
GROUPS = 4


def shifted(x, axis, by):
    count = lax.axis_size(axis)
    pairs = [(i, i + by) for i in range(count) if 0 <= i + by < count]
    return lax.ppermute(x, axis, pairs)


def butterfly_sum(x, axes):
    for axis in axes:
        count = lax.axis_size(axis)
        step = 1
        while step < count:
            x = x + lax.ppermute(x, axis, [(i, i ^ step) for i in range(count)])
            step = step * 2
    return x


def per_device(queries, keys, values, frames, upstream, lengths, conv_kernel):
    rows = queries.shape[0]
    channels = queries.shape[1]
    sub_count = lax.axis_size("sb")
    block_count_a = lax.axis_size("sa")
    group = channels // sub_count
    head_count = group // HEAD_DIM
    row_count = rows * sub_count
    span = row_count * block_count_a
    block_index = lax.axis_index("sa")
    group_index = lax.axis_index("sb")
    first_row = block_index * row_count
    length = lengths[0]
    score_scale = HEAD_DIM ** (-0.5)

    stacked = jnp.stack([queries, keys, values, frames, upstream])
    mixed = lax.all_to_all(
        stacked.reshape(5, rows, sub_count, group), "sb", 2, 1, tiled=True
    ).reshape(5, row_count, group)
    queries_b = mixed[0]
    frames_b = mixed[3]
    upstream_b = mixed[4]
    kv_all = lax.all_gather(
        jnp.concatenate([mixed[1], mixed[2]], axis=1), "sa", axis=0, tiled=True
    )
    key_all = kv_all[:, :group]
    value_all = kv_all[:, group:]

    key_block = row_count
    block_count = span // key_block
    key_blocks = key_all.reshape(block_count, key_block, head_count, HEAD_DIM)
    value_blocks = value_all.reshape(block_count, key_block, head_count, HEAD_DIM)
    block_starts = jnp.arange(block_count, dtype=jnp.int32) * key_block
    query_heads = queries_b.reshape(row_count, head_count, HEAD_DIM)

    def block_scores(key_part, block_start):
        scores = (
            jnp.einsum("thd,khd->htk", query_heads, key_part, preferred_element_type=jnp.float32)
            * score_scale
        )
        key_live = block_start + jnp.arange(key_part.shape[0], dtype=jnp.int32) < length
        return jnp.where(key_live[None, None, :], scores, -jnp.inf)

    def running_total(state_pair, block_items):
        running_top, total_sum = state_pair
        key_part, block_start = block_items
        scores = block_scores(key_part, block_start)
        higher = jnp.maximum(running_top, jnp.max(scores, axis=2))
        total_sum = total_sum * jnp.exp(running_top - higher) + jnp.sum(
            jnp.exp(scores - higher[:, :, None]), axis=2
        )
        return ((higher, total_sum), None)

    start_state = (
        jnp.full((head_count, row_count), -1e30, jnp.float32),
        jnp.zeros((head_count, row_count), jnp.float32),
    )
    (running_top, total_sum), unused = lax.scan(
        running_total, start_state, (key_blocks, block_starts)
    )
    log_total = running_top + jnp.log(total_sum)

    def attend_block(attend_acc, block_items):
        key_part, value_part, block_start = block_items
        prob_bf = jnp.exp(block_scores(key_part, block_start) - log_total[:, :, None]).astype(
            jnp.bfloat16
        )
        return (
            attend_acc
            + jnp.einsum("htk,khd->thd", prob_bf, value_part, preferred_element_type=jnp.float32),
            None,
        )

    attend_acc, unused = lax.scan(
        attend_block,
        jnp.zeros((row_count, head_count, HEAD_DIM), jnp.float32),
        (key_blocks, value_blocks, block_starts),
    )
    attended = attend_acc.reshape(row_count, group).astype(jnp.bfloat16)
    frame_live = (first_row + jnp.arange(row_count, dtype=jnp.int32) < length)[:, None]
    hidden = (frames_b.astype(jnp.float32) + attended.astype(jnp.float32)).astype(jnp.bfloat16)
    masked = jnp.where(frame_live, hidden, jnp.zeros_like(hidden))
    past_rows = shifted(masked[row_count - (KERNEL - 1) :], "sa", 1)
    extended = jnp.concatenate([past_rows, masked], axis=0).astype(jnp.float32)
    weights = lax.dynamic_slice_in_dim(conv_kernel, group_index * group, group, axis=1).astype(
        jnp.float32
    )
    conv_out = jnp.zeros((row_count, group), jnp.float32)
    for tap_index in range(KERNEL):
        conv_out = (
            conv_out
            + weights[tap_index]
            * extended[KERNEL - 1 - tap_index : KERNEL - 1 - tap_index + row_count]
        )
    sig_conv = jax.nn.sigmoid(conv_out)
    out = (hidden.astype(jnp.float32) + conv_out * sig_conv).astype(jnp.bfloat16)
    loss_grad = jnp.where(frame_live, upstream_b.astype(jnp.float32), 0.0)
    conv_grad = (loss_grad * sig_conv * (1.0 + conv_out * (1.0 - sig_conv))).astype(jnp.bfloat16)
    conv_float = conv_grad.astype(jnp.float32)
    kernel_part = jnp.stack(
        [
            jnp.sum(
                conv_float * extended[KERNEL - 1 - tap_index : KERNEL - 1 - tap_index + row_count],
                axis=0,
            )
            for tap_index in range(KERNEL)
        ]
    )
    future_rows = shifted(conv_grad[: KERNEL - 1], "sa", -1)
    ahead_rows = jnp.concatenate([conv_grad, future_rows], axis=0).astype(jnp.float32)
    back_conv = jnp.zeros((row_count, group), jnp.float32)
    for tap_index in range(KERNEL):
        back_conv = back_conv + weights[tap_index] * ahead_rows[tap_index : tap_index + row_count]
    frame_grad = (loss_grad + jnp.where(frame_live, back_conv, 0.0)).astype(jnp.bfloat16)
    grad_heads = frame_grad.reshape(row_count, head_count, HEAD_DIM)
    attended_heads = attended.reshape(row_count, head_count, HEAD_DIM)
    delta_rows = jnp.sum(
        grad_heads.astype(jnp.float32) * attended_heads.astype(jnp.float32), axis=2
    ).T

    def score_grads(key_part, value_part, block_start):
        soft_weights = jnp.exp(block_scores(key_part, block_start) - log_total[:, :, None])
        prob_grad = jnp.einsum(
            "thd,khd->htk", grad_heads, value_part, preferred_element_type=jnp.float32
        )
        score_grad = (soft_weights * (prob_grad - delta_rows[:, :, None])).astype(jnp.bfloat16)
        return (soft_weights.astype(jnp.bfloat16), score_grad)

    def gradient_block(query_acc, block_items):
        key_part, value_part, block_start = block_items
        prob_bf, score_grad = score_grads(key_part, value_part, block_start)
        query_acc = query_acc + jnp.einsum(
            "htk,khd->thd", score_grad, key_part, preferred_element_type=jnp.float32
        )
        key_term = (
            jnp.einsum("htk,thd->khd", score_grad, query_heads, preferred_element_type=jnp.float32)
            * score_scale
        )
        value_term = jnp.einsum(
            "htk,thd->khd", prob_bf, grad_heads, preferred_element_type=jnp.float32
        )
        grad_terms = jnp.concatenate(
            [key_term.reshape(key_block, group), value_term.reshape(key_block, group)], axis=1
        )
        return (query_acc, grad_terms)

    query_acc, grad_terms = lax.scan(
        gradient_block,
        jnp.zeros((row_count, head_count, HEAD_DIM), jnp.float32),
        (key_blocks, value_blocks, block_starts),
    )
    own_rows = lax.psum_scatter(
        grad_terms.reshape(span, 2 * group).astype(jnp.bfloat16),
        "sa",
        scatter_dimension=0,
        tiled=True,
    ).astype(jnp.float32)
    key_grad = own_rows[:, :group].astype(jnp.bfloat16)
    value_grad = own_rows[:, group:].astype(jnp.bfloat16)
    query_grad = (query_acc * score_scale).reshape(row_count, group).astype(jnp.bfloat16)
    kernel_full = lax.dynamic_update_slice_in_dim(
        jnp.zeros((KERNEL, channels), jnp.float32), kernel_part, group_index * group, axis=1
    )
    kernel_total = butterfly_sum(kernel_full, ("sb", "sa", "dp"))
    kernel_grad = kernel_total / lax.axis_size("dp")
    results = jnp.stack([out, query_grad, key_grad, value_grad, frame_grad])
    spread = lax.all_to_all(
        results.reshape(5, sub_count, rows, 1, group), "sb", 1, 3, tiled=True
    ).reshape(5, rows, channels)
    return (spread[0], spread[1], spread[2], spread[3], spread[4], kernel_grad)


def solution(mesh):
    seq_count = mesh.shape["seq"]
    split_mesh = Mesh(
        mesh.devices.reshape(mesh.shape["dp"], seq_count // GROUPS, GROUPS),
        ("dp", "sa", "sb"),
    )
    rows_spec = P(("dp", "sa", "sb"), None)
    placed = (rows_spec, rows_spec, rows_spec, rows_spec, rows_spec, P("dp"), P())
    return jax.shard_map(
        per_device,
        mesh=split_mesh,
        in_specs=placed,
        out_specs=(rows_spec, rows_spec, rows_spec, rows_spec, rows_spec, P()),
        check_vma=False,
    )
```

```python
import jax
import jax.numpy as jnp
from jax import lax
from jax.sharding import Mesh
from jax.sharding import PartitionSpec as P

HEAD_DIM = 64
KERNEL = 32
GROUPS = 4


def shifted(x, axis, by):
    count = lax.axis_size(axis)
    pairs = [(i, i + by) for i in range(count) if 0 <= i + by < count]
    return lax.ppermute(x, axis, pairs)


def radix_sum(x, axis):
    count = lax.axis_size(axis)
    position = lax.axis_index(axis)
    received = [x] + [
        lax.ppermute(x, axis, [(i, (i + s) % count) for i in range(count)])
        for s in range(1, count)
    ]
    ordered = jnp.stack(received)[(position - jnp.arange(count)) % count]
    total = ordered[0]
    for j in range(1, count):
        total = total + ordered[j]
    return total


def per_device(queries, keys, values, frames, upstream, lengths, conv_kernel):
    rows = queries.shape[0]
    channels = queries.shape[1]
    sub_count = lax.axis_size("sb")
    block_count_a = lax.axis_size("sa")
    group = channels // sub_count
    head_count = group // HEAD_DIM
    row_count = rows * sub_count
    span = row_count * block_count_a
    block_index = lax.axis_index("sa")
    group_index = lax.axis_index("sb")
    first_row = block_index * row_count
    length = lengths[0]
    score_scale = HEAD_DIM ** (-0.5)

    stacked = jnp.stack([queries, keys, values, frames, upstream])
    mixed = lax.all_to_all(
        stacked.reshape(5, rows, sub_count, group), "sb", 2, 1, tiled=True
    ).reshape(5, row_count, group)
    queries_b = mixed[0]
    frames_b = mixed[3]
    upstream_b = mixed[4]
    kv_local = jnp.concatenate([mixed[1], mixed[2]], axis=1)
    kv_parts = [kv_local] + [
        lax.ppermute(kv_local, "sa", [(i, (i + s) % block_count_a) for i in range(block_count_a)])
        for s in range(1, block_count_a)
    ]
    part_blocks = [(block_index - s) % block_count_a for s in range(block_count_a)]
    key_parts = [
        part[:, :group].reshape(row_count, head_count, HEAD_DIM) for part in kv_parts
    ]
    value_parts = [
        part[:, group:].reshape(row_count, head_count, HEAD_DIM) for part in kv_parts
    ]
    part_starts = [blk * row_count for blk in part_blocks]
    query_heads = queries_b.reshape(row_count, head_count, HEAD_DIM)

    def block_scores(key_part, block_start):
        scores = (
            jnp.einsum("thd,khd->htk", query_heads, key_part, preferred_element_type=jnp.float32)
            * score_scale
        )
        key_live = block_start + jnp.arange(key_part.shape[0], dtype=jnp.int32) < length
        return jnp.where(key_live[None, None, :], scores, -jnp.inf)

    running_top = jnp.full((head_count, row_count), -1e30, jnp.float32)
    total_sum = jnp.zeros((head_count, row_count), jnp.float32)
    for s in range(block_count_a):
        scores = block_scores(key_parts[s], part_starts[s])
        higher = jnp.maximum(running_top, jnp.max(scores, axis=2))
        total_sum = total_sum * jnp.exp(running_top - higher) + jnp.sum(
            jnp.exp(scores - higher[:, :, None]), axis=2
        )
        running_top = higher
    log_total = running_top + jnp.log(total_sum)

    attend_acc = jnp.zeros((row_count, head_count, HEAD_DIM), jnp.float32)
    for s in range(block_count_a):
        prob_bf = jnp.exp(block_scores(key_parts[s], part_starts[s]) - log_total[:, :, None]).astype(
            jnp.bfloat16
        )
        attend_acc = attend_acc + jnp.einsum(
            "htk,khd->thd", prob_bf, value_parts[s], preferred_element_type=jnp.float32
        )
    attended = attend_acc.reshape(row_count, group).astype(jnp.bfloat16)
    frame_live = (first_row + jnp.arange(row_count, dtype=jnp.int32) < length)[:, None]
    hidden = (frames_b.astype(jnp.float32) + attended.astype(jnp.float32)).astype(jnp.bfloat16)
    masked = jnp.where(frame_live, hidden, jnp.zeros_like(hidden))
    past_rows = shifted(masked[row_count - (KERNEL - 1) :], "sa", 1)
    extended = jnp.concatenate([past_rows, masked], axis=0).astype(jnp.float32)
    weights = lax.dynamic_slice_in_dim(conv_kernel, group_index * group, group, axis=1).astype(
        jnp.float32
    )
    conv_out = jnp.zeros((row_count, group), jnp.float32)
    for tap_index in range(KERNEL):
        conv_out = (
            conv_out
            + weights[tap_index]
            * extended[KERNEL - 1 - tap_index : KERNEL - 1 - tap_index + row_count]
        )
    sig_conv = jax.nn.sigmoid(conv_out)
    out = (hidden.astype(jnp.float32) + conv_out * sig_conv).astype(jnp.bfloat16)
    loss_grad = jnp.where(frame_live, upstream_b.astype(jnp.float32), 0.0)
    conv_grad = (loss_grad * sig_conv * (1.0 + conv_out * (1.0 - sig_conv))).astype(jnp.bfloat16)
    conv_float = conv_grad.astype(jnp.float32)
    kernel_part = jnp.stack(
        [
            jnp.sum(
                conv_float * extended[KERNEL - 1 - tap_index : KERNEL - 1 - tap_index + row_count],
                axis=0,
            )
            for tap_index in range(KERNEL)
        ]
    )
    future_rows = shifted(conv_grad[: KERNEL - 1], "sa", -1)
    ahead_rows = jnp.concatenate([conv_grad, future_rows], axis=0).astype(jnp.float32)
    back_conv = jnp.zeros((row_count, group), jnp.float32)
    for tap_index in range(KERNEL):
        back_conv = back_conv + weights[tap_index] * ahead_rows[tap_index : tap_index + row_count]
    frame_grad = (loss_grad + jnp.where(frame_live, back_conv, 0.0)).astype(jnp.bfloat16)
    grad_heads = frame_grad.reshape(row_count, head_count, HEAD_DIM)
    attended_heads = attended.reshape(row_count, head_count, HEAD_DIM)
    delta_rows = jnp.sum(
        grad_heads.astype(jnp.float32) * attended_heads.astype(jnp.float32), axis=2
    ).T

    def score_grads(key_part, value_part, block_start):
        soft_weights = jnp.exp(block_scores(key_part, block_start) - log_total[:, :, None])
        prob_grad = jnp.einsum(
            "thd,khd->htk", grad_heads, value_part, preferred_element_type=jnp.float32
        )
        score_grad = (soft_weights * (prob_grad - delta_rows[:, :, None])).astype(jnp.bfloat16)
        return (soft_weights.astype(jnp.bfloat16), score_grad)

    query_acc = jnp.zeros((row_count, head_count, HEAD_DIM), jnp.float32)
    own_terms = None
    arrived = []
    kernel_rounds = [
        lambda value: radix_sum(value, "sa"),
        lambda value: radix_sum(value, "dp"),
        lambda value: radix_sum(
            lax.dynamic_update_slice_in_dim(
                jnp.zeros((KERNEL, channels), jnp.float32), value, group_index * group, axis=1
            ),
            "sb",
        ),
    ]
    kernel_sum = kernel_part
    for step, s in enumerate(list(range(1, block_count_a)) + [0]):
        if step < len(kernel_rounds):
            kernel_sum = kernel_rounds[step](kernel_sum)
        key_part = key_parts[s]
        prob_bf, score_grad = score_grads(key_part, value_parts[s], part_starts[s])
        query_acc = query_acc + jnp.einsum(
            "htk,khd->thd", score_grad, key_part, preferred_element_type=jnp.float32
        )
        key_term = (
            jnp.einsum("htk,thd->khd", score_grad, query_heads, preferred_element_type=jnp.float32)
            * score_scale
        )
        value_term = jnp.einsum(
            "htk,thd->khd", prob_bf, grad_heads, preferred_element_type=jnp.float32
        )
        grad_terms = jnp.concatenate(
            [key_term.reshape(row_count, group), value_term.reshape(row_count, group)], axis=1
        ).astype(jnp.bfloat16)
        if step < len(kernel_rounds):
            kernel_sum, query_acc = lax.optimization_barrier((kernel_sum, query_acc))
        if s == 0:
            own_terms = grad_terms
        else:
            arrived.append(
                lax.ppermute(
                    grad_terms,
                    "sa",
                    [(i, (i - s) % block_count_a) for i in range(block_count_a)],
                )
            )
    own_rows = own_terms.astype(jnp.float32)
    for part in arrived:
        own_rows = own_rows + part.astype(jnp.float32)
    key_grad = own_rows[:, :group].astype(jnp.bfloat16)
    value_grad = own_rows[:, group:].astype(jnp.bfloat16)
    query_grad = (query_acc * score_scale).reshape(row_count, group).astype(jnp.bfloat16)
    kernel_total = kernel_sum
    kernel_grad = kernel_total / lax.axis_size("dp")
    results = jnp.stack([out, query_grad, key_grad, value_grad, frame_grad])
    spread = lax.all_to_all(
        results.reshape(5, sub_count, rows, 1, group), "sb", 1, 3, tiled=True
    ).reshape(5, rows, channels)
    return (spread[0], spread[1], spread[2], spread[3], spread[4], kernel_grad)


def solution(mesh):
    seq_count = mesh.shape["seq"]
    split_mesh = Mesh(
        mesh.devices.reshape(mesh.shape["dp"], seq_count // GROUPS, GROUPS),
        ("dp", "sa", "sb"),
    )
    rows_spec = P(("dp", "sa", "sb"), None)
    placed = (rows_spec, rows_spec, rows_spec, rows_spec, rows_spec, P("dp"), P())
    return jax.shard_map(
        per_device,
        mesh=split_mesh,
        in_specs=placed,
        out_specs=(rows_spec, rows_spec, rows_spec, rows_spec, rows_spec, P()),
        check_vma=False,
    )
```

```python
import jax
import jax.numpy as jnp
from jax import lax
from jax.sharding import Mesh
from jax.sharding import PartitionSpec as P

HEAD_DIM = 64
KERNEL = 32
GROUPS = 4


def shifted(x, axis, by):
    count = lax.axis_size(axis)
    pairs = [(i, i + by) for i in range(count) if 0 <= i + by < count]
    return lax.ppermute(x, axis, pairs)


def radix_sum(x, axis):
    count = lax.axis_size(axis)
    position = lax.axis_index(axis)
    received = [x] + [
        lax.ppermute(x, axis, [(i, (i + s) % count) for i in range(count)])
        for s in range(1, count)
    ]
    ordered = jnp.stack(received)[(position - jnp.arange(count)) % count]
    total = ordered[0]
    for j in range(1, count):
        total = total + ordered[j]
    return total


def xor_step(x, axis, step):
    count = lax.axis_size(axis)
    return x + lax.ppermute(x, axis, [(i, i ^ step) for i in range(count)])


def to_blocks(x, rows, sub_count, group):
    return lax.all_to_all(x.reshape(rows, sub_count, group), "sb", 1, 0, tiled=True).reshape(
        rows * sub_count, group
    )


def to_rows(y, rows, sub_count, group):
    return lax.all_to_all(y.reshape(sub_count, rows, 1, group), "sb", 0, 2, tiled=True).reshape(
        rows, sub_count * group
    )


def per_device(queries, keys, values, frames, upstream, lengths, conv_kernel):
    rows = queries.shape[0]
    channels = queries.shape[1]
    sub_count = lax.axis_size("sb")
    block_count_a = lax.axis_size("sa")
    group = channels // sub_count
    head_count = group // HEAD_DIM
    row_count = rows * sub_count
    span = row_count * block_count_a
    block_index = lax.axis_index("sa")
    group_index = lax.axis_index("sb")
    first_row = block_index * row_count
    length = lengths[0]
    score_scale = HEAD_DIM ** (-0.5)

    queries_b = to_blocks(queries, rows, sub_count, group)
    keys_b = to_blocks(keys, rows, sub_count, group)
    values_b = to_blocks(values, rows, sub_count, group)
    frames_b = to_blocks(frames, rows, sub_count, group)
    upstream_b = to_blocks(upstream, rows, sub_count, group)
    shifts = [[(i, (i + s) % block_count_a) for i in range(block_count_a)] for s in range(1, block_count_a)]
    key_recv = [lax.ppermute(keys_b, "sa", pairs) for pairs in shifts]
    key_recv_tied, values_tied = lax.optimization_barrier((key_recv, values_b))
    value_recv = [lax.ppermute(values_tied, "sa", pairs) for pairs in shifts]
    key_flat = [keys_b] + list(key_recv_tied)
    value_flat = [values_b] + value_recv
    part_blocks = [(block_index - s) % block_count_a for s in range(block_count_a)]
    key_parts = [part.reshape(row_count, head_count, HEAD_DIM) for part in key_flat]
    value_parts = [part.reshape(row_count, head_count, HEAD_DIM) for part in value_flat]
    part_starts = [blk * row_count for blk in part_blocks]
    query_heads = queries_b.reshape(row_count, head_count, HEAD_DIM)

    def block_scores(key_part, block_start):
        scores = (
            jnp.einsum("thd,khd->htk", query_heads, key_part, preferred_element_type=jnp.float32)
            * score_scale
        )
        key_live = block_start + jnp.arange(key_part.shape[0], dtype=jnp.int32) < length
        return jnp.where(key_live[None, None, :], scores, -jnp.inf)

    running_top = jnp.full((head_count, row_count), -1e30, jnp.float32)
    total_sum = jnp.zeros((head_count, row_count), jnp.float32)
    for s in range(block_count_a):
        scores = block_scores(key_parts[s], part_starts[s])
        higher = jnp.maximum(running_top, jnp.max(scores, axis=2))
        total_sum = total_sum * jnp.exp(running_top - higher) + jnp.sum(
            jnp.exp(scores - higher[:, :, None]), axis=2
        )
        running_top = higher
    log_total = running_top + jnp.log(total_sum)

    attend_acc = jnp.zeros((row_count, head_count, HEAD_DIM), jnp.float32)
    for s in range(block_count_a):
        prob_bf = jnp.exp(block_scores(key_parts[s], part_starts[s]) - log_total[:, :, None]).astype(
            jnp.bfloat16
        )
        attend_acc = attend_acc + jnp.einsum(
            "htk,khd->thd", prob_bf, value_parts[s], preferred_element_type=jnp.float32
        )
    attended = attend_acc.reshape(row_count, group).astype(jnp.bfloat16)
    frame_live = (first_row + jnp.arange(row_count, dtype=jnp.int32) < length)[:, None]
    hidden = (frames_b.astype(jnp.float32) + attended.astype(jnp.float32)).astype(jnp.bfloat16)
    masked = jnp.where(frame_live, hidden, jnp.zeros_like(hidden))
    past_rows = shifted(masked[row_count - (KERNEL - 1) :], "sa", 1)
    extended = jnp.concatenate([past_rows, masked], axis=0).astype(jnp.float32)
    weights = lax.dynamic_slice_in_dim(conv_kernel, group_index * group, group, axis=1).astype(
        jnp.float32
    )
    conv_out = jnp.zeros((row_count, group), jnp.float32)
    for tap_index in range(KERNEL):
        conv_out = (
            conv_out
            + weights[tap_index]
            * extended[KERNEL - 1 - tap_index : KERNEL - 1 - tap_index + row_count]
        )
    sig_conv = jax.nn.sigmoid(conv_out)
    out = (hidden.astype(jnp.float32) + conv_out * sig_conv).astype(jnp.bfloat16)
    loss_grad = jnp.where(frame_live, upstream_b.astype(jnp.float32), 0.0)
    conv_grad = (loss_grad * sig_conv * (1.0 + conv_out * (1.0 - sig_conv))).astype(jnp.bfloat16)
    conv_float = conv_grad.astype(jnp.float32)
    kernel_part = jnp.stack(
        [
            jnp.sum(
                conv_float * extended[KERNEL - 1 - tap_index : KERNEL - 1 - tap_index + row_count],
                axis=0,
            )
            for tap_index in range(KERNEL)
        ]
    )
    future_rows = shifted(conv_grad[: KERNEL - 1], "sa", -1)
    ahead_rows = jnp.concatenate([conv_grad, future_rows], axis=0).astype(jnp.float32)
    back_conv = jnp.zeros((row_count, group), jnp.float32)
    for tap_index in range(KERNEL):
        back_conv = back_conv + weights[tap_index] * ahead_rows[tap_index : tap_index + row_count]
    frame_grad = (loss_grad + jnp.where(frame_live, back_conv, 0.0)).astype(jnp.bfloat16)
    grad_heads = frame_grad.reshape(row_count, head_count, HEAD_DIM)
    attended_heads = attended.reshape(row_count, head_count, HEAD_DIM)
    delta_rows = jnp.sum(
        grad_heads.astype(jnp.float32) * attended_heads.astype(jnp.float32), axis=2
    ).T

    def score_grads(key_part, value_part, block_start):
        soft_weights = jnp.exp(block_scores(key_part, block_start) - log_total[:, :, None])
        prob_grad = jnp.einsum(
            "thd,khd->htk", grad_heads, value_part, preferred_element_type=jnp.float32
        )
        score_grad = (soft_weights * (prob_grad - delta_rows[:, :, None])).astype(jnp.bfloat16)
        return (soft_weights.astype(jnp.bfloat16), score_grad)

    query_acc = jnp.zeros((row_count, head_count, HEAD_DIM), jnp.float32)
    own_terms = None
    arrived = []
    kernel_rounds = [
        lambda value: radix_sum(value, "sa"),
        lambda value: xor_step(xor_step(value, "dp", 1), "dp", 2),
        lambda value: xor_step(xor_step(value, "dp", 4), "dp", 8),
        lambda value: radix_sum(
            lax.dynamic_update_slice_in_dim(
                jnp.zeros((KERNEL, channels), jnp.float32), value, group_index * group, axis=1
            ),
            "sb",
        ),
    ]
    kernel_sum = kernel_part
    for step, s in enumerate(list(range(1, block_count_a)) + [0]):
        kernel_sum = kernel_rounds[step](kernel_sum)
        key_part = key_parts[s]
        value_part = value_parts[s]
        if step > 0:
            kernel_sum, key_part, value_part = lax.optimization_barrier(
                (kernel_sum, key_part, value_part)
            )
        prob_bf, score_grad = score_grads(key_part, value_part, part_starts[s])
        query_acc = query_acc + jnp.einsum(
            "htk,khd->thd", score_grad, key_part, preferred_element_type=jnp.float32
        )
        key_term = (
            jnp.einsum("htk,thd->khd", score_grad, query_heads, preferred_element_type=jnp.float32)
            * score_scale
        )
        value_term = jnp.einsum(
            "htk,thd->khd", prob_bf, grad_heads, preferred_element_type=jnp.float32
        )
        grad_terms = jnp.concatenate(
            [key_term.reshape(row_count, group), value_term.reshape(row_count, group)], axis=1
        ).astype(jnp.bfloat16)
        if s == 0:
            own_terms = grad_terms
        else:
            arrived.append(
                lax.ppermute(
                    grad_terms,
                    "sa",
                    [(i, (i - s) % block_count_a) for i in range(block_count_a)],
                )
            )
    own_rows = own_terms.astype(jnp.float32)
    for part in arrived:
        own_rows = own_rows + part.astype(jnp.float32)
    key_grad = own_rows[:, :group].astype(jnp.bfloat16)
    value_grad = own_rows[:, group:].astype(jnp.bfloat16)
    query_grad = (query_acc * score_scale).reshape(row_count, group).astype(jnp.bfloat16)
    kernel_total = kernel_sum
    kernel_grad = kernel_total / lax.axis_size("dp")
    return (
        to_rows(out, rows, sub_count, group),
        to_rows(query_grad, rows, sub_count, group),
        to_rows(key_grad, rows, sub_count, group),
        to_rows(value_grad, rows, sub_count, group),
        to_rows(frame_grad, rows, sub_count, group),
        kernel_grad,
    )


def solution(mesh):
    seq_count = mesh.shape["seq"]
    split_mesh = Mesh(
        mesh.devices.reshape(mesh.shape["dp"], seq_count // GROUPS, GROUPS),
        ("dp", "sa", "sb"),
    )
    rows_spec = P(("dp", "sa", "sb"), None)
    placed = (rows_spec, rows_spec, rows_spec, rows_spec, rows_spec, P("dp"), P())
    return jax.shard_map(
        per_device,
        mesh=split_mesh,
        in_specs=placed,
        out_specs=(rows_spec, rows_spec, rows_spec, rows_spec, rows_spec, P()),
        check_vma=False,
    )
```

```python
import jax
import jax.numpy as jnp
from jax import lax
from jax.sharding import Mesh
from jax.sharding import PartitionSpec as P

HEAD_DIM = 64
KERNEL = 32
GROUPS = 4


def shifted(x, axis, by):
    count = lax.axis_size(axis)
    pairs = [(i, i + by) for i in range(count) if 0 <= i + by < count]
    return lax.ppermute(x, axis, pairs)


def radix_sum(x, axis):
    count = lax.axis_size(axis)
    position = lax.axis_index(axis)
    received = [x] + [
        lax.ppermute(x, axis, [(i, (i + s) % count) for i in range(count)])
        for s in range(1, count)
    ]
    ordered = jnp.stack(received)[(position - jnp.arange(count)) % count]
    total = ordered[0]
    for j in range(1, count):
        total = total + ordered[j]
    return total


def xor_step(x, axis, step):
    count = lax.axis_size(axis)
    return x + lax.ppermute(x, axis, [(i, i ^ step) for i in range(count)])


def to_blocks(x, rows, sub_count, group):
    return lax.all_to_all(x.reshape(rows, sub_count, group), "sb", 1, 0, tiled=True).reshape(
        rows * sub_count, group
    )


def to_rows(y, rows, sub_count, group):
    return lax.all_to_all(y.reshape(sub_count, rows, 1, group), "sb", 0, 2, tiled=True).reshape(
        rows, sub_count * group
    )


def per_device(queries, keys, values, frames, upstream, lengths, conv_kernel):
    rows = queries.shape[0]
    channels = queries.shape[1]
    sub_count = lax.axis_size("sb")
    block_count_a = lax.axis_size("sa")
    group = channels // sub_count
    head_count = group // HEAD_DIM
    row_count = rows * sub_count
    span = row_count * block_count_a
    block_index = lax.axis_index("sa")
    group_index = lax.axis_index("sb")
    first_row = block_index * row_count
    length = lengths[0]
    score_scale = HEAD_DIM ** (-0.5)

    keys_b = to_blocks(keys, rows, sub_count, group)
    rest = lax.all_to_all(
        jnp.stack([queries, values, frames, upstream]).reshape(4, rows, sub_count, group),
        "sb",
        2,
        1,
        tiled=True,
    ).reshape(4, row_count, group)
    queries_b = rest[0]
    values_b = rest[1]
    frames_b = rest[2]
    upstream_b = rest[3]
    shifts = [[(i, (i + s) % block_count_a) for i in range(block_count_a)] for s in range(1, block_count_a)]
    key_recv = [lax.ppermute(keys_b, "sa", pairs) for pairs in shifts]
    key_recv_tied, values_tied = lax.optimization_barrier((key_recv, values_b))
    value_recv = [lax.ppermute(values_tied, "sa", pairs) for pairs in shifts]
    key_flat = [keys_b] + list(key_recv_tied)
    value_flat = [values_b] + value_recv
    part_blocks = [(block_index - s) % block_count_a for s in range(block_count_a)]
    key_parts = [part.reshape(row_count, head_count, HEAD_DIM) for part in key_flat]
    value_parts = [part.reshape(row_count, head_count, HEAD_DIM) for part in value_flat]
    part_starts = [blk * row_count for blk in part_blocks]
    query_heads = queries_b.reshape(row_count, head_count, HEAD_DIM)

    def block_scores(key_part, block_start):
        scores = (
            jnp.einsum("thd,khd->htk", query_heads, key_part, preferred_element_type=jnp.float32)
            * score_scale
        )
        key_live = block_start + jnp.arange(key_part.shape[0], dtype=jnp.int32) < length
        return jnp.where(key_live[None, None, :], scores, -jnp.inf)

    running_top = jnp.full((head_count, row_count), -1e30, jnp.float32)
    total_sum = jnp.zeros((head_count, row_count), jnp.float32)
    for s in range(block_count_a):
        scores = block_scores(key_parts[s], part_starts[s])
        higher = jnp.maximum(running_top, jnp.max(scores, axis=2))
        total_sum = total_sum * jnp.exp(running_top - higher) + jnp.sum(
            jnp.exp(scores - higher[:, :, None]), axis=2
        )
        running_top = higher
    log_total = running_top + jnp.log(total_sum)

    attend_acc = jnp.zeros((row_count, head_count, HEAD_DIM), jnp.float32)
    for s in range(block_count_a):
        prob_bf = jnp.exp(block_scores(key_parts[s], part_starts[s]) - log_total[:, :, None]).astype(
            jnp.bfloat16
        )
        attend_acc = attend_acc + jnp.einsum(
            "htk,khd->thd", prob_bf, value_parts[s], preferred_element_type=jnp.float32
        )
    attended = attend_acc.reshape(row_count, group).astype(jnp.bfloat16)
    frame_live = (first_row + jnp.arange(row_count, dtype=jnp.int32) < length)[:, None]
    hidden = (frames_b.astype(jnp.float32) + attended.astype(jnp.float32)).astype(jnp.bfloat16)
    masked = jnp.where(frame_live, hidden, jnp.zeros_like(hidden))
    past_rows = shifted(masked[row_count - (KERNEL - 1) :], "sa", 1)
    extended = jnp.concatenate([past_rows, masked], axis=0).astype(jnp.float32)
    weights = lax.dynamic_slice_in_dim(conv_kernel, group_index * group, group, axis=1).astype(
        jnp.float32
    )
    conv_out = jnp.zeros((row_count, group), jnp.float32)
    for tap_index in range(KERNEL):
        conv_out = (
            conv_out
            + weights[tap_index]
            * extended[KERNEL - 1 - tap_index : KERNEL - 1 - tap_index + row_count]
        )
    sig_conv = jax.nn.sigmoid(conv_out)
    out = (hidden.astype(jnp.float32) + conv_out * sig_conv).astype(jnp.bfloat16)
    loss_grad = jnp.where(frame_live, upstream_b.astype(jnp.float32), 0.0)
    conv_grad = (loss_grad * sig_conv * (1.0 + conv_out * (1.0 - sig_conv))).astype(jnp.bfloat16)
    conv_float = conv_grad.astype(jnp.float32)
    kernel_part = jnp.stack(
        [
            jnp.sum(
                conv_float * extended[KERNEL - 1 - tap_index : KERNEL - 1 - tap_index + row_count],
                axis=0,
            )
            for tap_index in range(KERNEL)
        ]
    )
    future_rows = shifted(conv_grad[: KERNEL - 1], "sa", -1)
    ahead_rows = jnp.concatenate([conv_grad, future_rows], axis=0).astype(jnp.float32)
    back_conv = jnp.zeros((row_count, group), jnp.float32)
    for tap_index in range(KERNEL):
        back_conv = back_conv + weights[tap_index] * ahead_rows[tap_index : tap_index + row_count]
    frame_grad = (loss_grad + jnp.where(frame_live, back_conv, 0.0)).astype(jnp.bfloat16)
    grad_heads = frame_grad.reshape(row_count, head_count, HEAD_DIM)
    attended_heads = attended.reshape(row_count, head_count, HEAD_DIM)
    delta_rows = jnp.sum(
        grad_heads.astype(jnp.float32) * attended_heads.astype(jnp.float32), axis=2
    ).T

    def score_grads(key_part, value_part, block_start):
        soft_weights = jnp.exp(block_scores(key_part, block_start) - log_total[:, :, None])
        prob_grad = jnp.einsum(
            "thd,khd->htk", grad_heads, value_part, preferred_element_type=jnp.float32
        )
        score_grad = (soft_weights * (prob_grad - delta_rows[:, :, None])).astype(jnp.bfloat16)
        return (soft_weights.astype(jnp.bfloat16), score_grad)

    query_acc = jnp.zeros((row_count, head_count, HEAD_DIM), jnp.float32)
    own_terms = None
    arrived = []
    kernel_rounds = [
        lambda value: radix_sum(value, "sa"),
        lambda value: xor_step(xor_step(value, "dp", 1), "dp", 2),
        lambda value: xor_step(xor_step(value, "dp", 4), "dp", 8),
        lambda value: radix_sum(
            lax.dynamic_update_slice_in_dim(
                jnp.zeros((KERNEL, channels), jnp.float32), value, group_index * group, axis=1
            ),
            "sb",
        ),
    ]
    kernel_sum = kernel_part
    for step, s in enumerate(list(range(1, block_count_a)) + [0]):
        kernel_sum = kernel_rounds[step](kernel_sum)
        key_part = key_parts[s]
        value_part = value_parts[s]
        if step > 0:
            kernel_sum, key_part, value_part = lax.optimization_barrier(
                (kernel_sum, key_part, value_part)
            )
        prob_bf, score_grad = score_grads(key_part, value_part, part_starts[s])
        query_acc = query_acc + jnp.einsum(
            "htk,khd->thd", score_grad, key_part, preferred_element_type=jnp.float32
        )
        key_term = (
            jnp.einsum("htk,thd->khd", score_grad, query_heads, preferred_element_type=jnp.float32)
            * score_scale
        )
        value_term = jnp.einsum(
            "htk,thd->khd", prob_bf, grad_heads, preferred_element_type=jnp.float32
        )
        grad_terms = jnp.concatenate(
            [key_term.reshape(row_count, group), value_term.reshape(row_count, group)], axis=1
        ).astype(jnp.bfloat16)
        if s == 0:
            own_terms = grad_terms
        else:
            arrived.append(
                lax.ppermute(
                    grad_terms,
                    "sa",
                    [(i, (i - s) % block_count_a) for i in range(block_count_a)],
                )
            )
    own_rows = own_terms.astype(jnp.float32)
    for part in arrived:
        own_rows = own_rows + part.astype(jnp.float32)
    key_grad = own_rows[:, :group].astype(jnp.bfloat16)
    value_grad = own_rows[:, group:].astype(jnp.bfloat16)
    query_grad = (query_acc * score_scale).reshape(row_count, group).astype(jnp.bfloat16)
    kernel_total = kernel_sum
    kernel_grad = kernel_total / lax.axis_size("dp")
    early = lax.all_to_all(
        jnp.stack([out, frame_grad]).reshape(2, sub_count, rows, 1, group), "sb", 1, 3, tiled=True
    ).reshape(2, rows, channels)
    late = lax.all_to_all(
        jnp.stack([query_grad, key_grad, value_grad]).reshape(3, sub_count, rows, 1, group),
        "sb",
        1,
        3,
        tiled=True,
    ).reshape(3, rows, channels)
    return (early[0], late[0], late[1], late[2], early[1], kernel_grad)


def solution(mesh):
    seq_count = mesh.shape["seq"]
    split_mesh = Mesh(
        mesh.devices.reshape(mesh.shape["dp"], seq_count // GROUPS, GROUPS),
        ("dp", "sa", "sb"),
    )
    rows_spec = P(("dp", "sa", "sb"), None)
    placed = (rows_spec, rows_spec, rows_spec, rows_spec, rows_spec, P("dp"), P())
    return jax.shard_map(
        per_device,
        mesh=split_mesh,
        in_specs=placed,
        out_specs=(rows_spec, rows_spec, rows_spec, rows_spec, rows_spec, P()),
        check_vma=False,
    )
```

```python
import jax
import jax.numpy as jnp
from jax import lax
from jax.sharding import Mesh
from jax.sharding import PartitionSpec as P

HEAD_DIM = 64
KERNEL = 32
GROUPS = 4


def shifted(x, axis, by):
    count = lax.axis_size(axis)
    pairs = [(i, i + by) for i in range(count) if 0 <= i + by < count]
    return lax.ppermute(x, axis, pairs)


def radix_sum(x, axis):
    count = lax.axis_size(axis)
    position = lax.axis_index(axis)
    received = [x] + [
        lax.ppermute(x, axis, [(i, (i + s) % count) for i in range(count)])
        for s in range(1, count)
    ]
    ordered = jnp.stack(received)[(position - jnp.arange(count)) % count]
    total = ordered[0]
    for j in range(1, count):
        total = total + ordered[j]
    return total


def xor_step(x, axis, step):
    count = lax.axis_size(axis)
    return x + lax.ppermute(x, axis, [(i, i ^ step) for i in range(count)])


def to_blocks(x, rows, sub_count, group):
    return lax.all_to_all(x.reshape(rows, sub_count, group), "sb", 1, 0, tiled=True).reshape(
        rows * sub_count, group
    )


def to_rows(y, rows, sub_count, group):
    return lax.all_to_all(y.reshape(sub_count, rows, 1, group), "sb", 0, 2, tiled=True).reshape(
        rows, sub_count * group
    )


def per_device(queries, keys, values, frames, upstream, lengths, conv_kernel):
    rows = queries.shape[0]
    channels = queries.shape[1]
    sub_count = lax.axis_size("sb")
    block_count_a = lax.axis_size("sa")
    group = channels // sub_count
    head_count = group // HEAD_DIM
    row_count = rows * sub_count
    span = row_count * block_count_a
    block_index = lax.axis_index("sa")
    group_index = lax.axis_index("sb")
    first_row = block_index * row_count
    length = lengths[0]
    score_scale = HEAD_DIM ** (-0.5)

    keys_b = to_blocks(keys, rows, sub_count, group)
    rest = lax.all_to_all(
        jnp.stack([queries, values, frames, upstream]).reshape(4, rows, sub_count, group),
        "sb",
        2,
        1,
        tiled=True,
    ).reshape(4, row_count, group)
    queries_b = rest[0]
    values_b = rest[1]
    frames_b = rest[2]
    upstream_b = rest[3]
    shifts = [[(i, (i + s) % block_count_a) for i in range(block_count_a)] for s in range(1, block_count_a)]
    key_recv = [lax.ppermute(keys_b, "sa", pairs) for pairs in shifts]
    key_recv_tied, values_tied = lax.optimization_barrier((key_recv, values_b))
    value_recv = [lax.ppermute(values_tied, "sa", pairs) for pairs in shifts]
    key_flat = [keys_b] + list(key_recv_tied)
    value_flat = [values_b] + value_recv
    part_blocks = [(block_index - s) % block_count_a for s in range(block_count_a)]
    key_parts = [part.reshape(row_count, head_count, HEAD_DIM) for part in key_flat]
    value_parts = [part.reshape(row_count, head_count, HEAD_DIM) for part in value_flat]
    part_starts = [blk * row_count for blk in part_blocks]
    query_heads = queries_b.reshape(row_count, head_count, HEAD_DIM)

    def block_scores(key_part, block_start):
        scores = (
            jnp.einsum("thd,khd->htk", query_heads, key_part, preferred_element_type=jnp.float32)
            * score_scale
        )
        key_live = block_start + jnp.arange(key_part.shape[0], dtype=jnp.int32) < length
        return jnp.where(key_live[None, None, :], scores, -jnp.inf)

    running_top = jnp.full((head_count, row_count), -1e30, jnp.float32)
    total_sum = jnp.zeros((head_count, row_count), jnp.float32)
    score_list = []
    for s in range(block_count_a):
        scores = block_scores(key_parts[s], part_starts[s])
        score_list.append(scores)
        higher = jnp.maximum(running_top, jnp.max(scores, axis=2))
        total_sum = total_sum * jnp.exp(running_top - higher) + jnp.sum(
            jnp.exp(scores - higher[:, :, None]), axis=2
        )
        running_top = higher
    log_total = running_top + jnp.log(total_sum)

    attend_acc = jnp.zeros((row_count, head_count, HEAD_DIM), jnp.float32)
    for s in range(block_count_a):
        prob_bf = jnp.exp(score_list[s] - log_total[:, :, None]).astype(
            jnp.bfloat16
        )
        attend_acc = attend_acc + jnp.einsum(
            "htk,khd->thd", prob_bf, value_parts[s], preferred_element_type=jnp.float32
        )
    attended = attend_acc.reshape(row_count, group).astype(jnp.bfloat16)
    frame_live = (first_row + jnp.arange(row_count, dtype=jnp.int32) < length)[:, None]
    hidden = (frames_b.astype(jnp.float32) + attended.astype(jnp.float32)).astype(jnp.bfloat16)
    masked = jnp.where(frame_live, hidden, jnp.zeros_like(hidden))
    past_rows = shifted(masked[row_count - (KERNEL - 1) :], "sa", 1)
    extended = jnp.concatenate([past_rows, masked], axis=0).astype(jnp.float32)
    weights = lax.dynamic_slice_in_dim(conv_kernel, group_index * group, group, axis=1).astype(
        jnp.float32
    )
    conv_out = jnp.zeros((row_count, group), jnp.float32)
    for tap_index in range(KERNEL):
        conv_out = (
            conv_out
            + weights[tap_index]
            * extended[KERNEL - 1 - tap_index : KERNEL - 1 - tap_index + row_count]
        )
    sig_conv = jax.nn.sigmoid(conv_out)
    out = (hidden.astype(jnp.float32) + conv_out * sig_conv).astype(jnp.bfloat16)
    loss_grad = jnp.where(frame_live, upstream_b.astype(jnp.float32), 0.0)
    conv_grad = (loss_grad * sig_conv * (1.0 + conv_out * (1.0 - sig_conv))).astype(jnp.bfloat16)
    conv_float = conv_grad.astype(jnp.float32)
    kernel_part = jnp.stack(
        [
            jnp.sum(
                conv_float * extended[KERNEL - 1 - tap_index : KERNEL - 1 - tap_index + row_count],
                axis=0,
            )
            for tap_index in range(KERNEL)
        ]
    )
    future_rows = shifted(conv_grad[: KERNEL - 1], "sa", -1)
    ahead_rows = jnp.concatenate([conv_grad, future_rows], axis=0).astype(jnp.float32)
    back_conv = jnp.zeros((row_count, group), jnp.float32)
    for tap_index in range(KERNEL):
        back_conv = back_conv + weights[tap_index] * ahead_rows[tap_index : tap_index + row_count]
    frame_grad = (loss_grad + jnp.where(frame_live, back_conv, 0.0)).astype(jnp.bfloat16)
    grad_heads = frame_grad.reshape(row_count, head_count, HEAD_DIM)
    attended_heads = attended.reshape(row_count, head_count, HEAD_DIM)
    delta_rows = jnp.sum(
        grad_heads.astype(jnp.float32) * attended_heads.astype(jnp.float32), axis=2
    ).T

    def score_grads(scores, value_part):
        soft_weights = jnp.exp(scores - log_total[:, :, None])
        prob_grad = jnp.einsum(
            "thd,khd->htk", grad_heads, value_part, preferred_element_type=jnp.float32
        )
        score_grad = (soft_weights * (prob_grad - delta_rows[:, :, None])).astype(jnp.bfloat16)
        return (soft_weights.astype(jnp.bfloat16), score_grad)

    query_acc = jnp.zeros((row_count, head_count, HEAD_DIM), jnp.float32)
    own_terms = None
    arrived = []
    kernel_rounds = [
        lambda value: radix_sum(value, "sa"),
        lambda value: xor_step(xor_step(value, "dp", 1), "dp", 2),
        lambda value: xor_step(xor_step(value, "dp", 4), "dp", 8),
        lambda value: radix_sum(
            lax.dynamic_update_slice_in_dim(
                jnp.zeros((KERNEL, channels), jnp.float32), value, group_index * group, axis=1
            ),
            "sb",
        ),
    ]
    kernel_sum = kernel_part
    for step, s in enumerate(list(range(1, block_count_a)) + [0]):
        kernel_sum = kernel_rounds[step](kernel_sum)
        key_part = key_parts[s]
        value_part = value_parts[s]
        if step > 0:
            kernel_sum, key_part, value_part = lax.optimization_barrier(
                (kernel_sum, key_part, value_part)
            )
        prob_bf, score_grad = score_grads(score_list[s], value_part)
        query_acc = query_acc + jnp.einsum(
            "htk,khd->thd", score_grad, key_part, preferred_element_type=jnp.float32
        )
        key_term = (
            jnp.einsum("htk,thd->khd", score_grad, query_heads, preferred_element_type=jnp.float32)
            * score_scale
        )
        value_term = jnp.einsum(
            "htk,thd->khd", prob_bf, grad_heads, preferred_element_type=jnp.float32
        )
        grad_terms = jnp.concatenate(
            [key_term.reshape(row_count, group), value_term.reshape(row_count, group)], axis=1
        ).astype(jnp.bfloat16)
        if s == 0:
            own_terms = grad_terms
        else:
            arrived.append(
                lax.ppermute(
                    grad_terms,
                    "sa",
                    [(i, (i - s) % block_count_a) for i in range(block_count_a)],
                )
            )
    own_rows = own_terms.astype(jnp.float32)
    for part in arrived:
        own_rows = own_rows + part.astype(jnp.float32)
    key_grad = own_rows[:, :group].astype(jnp.bfloat16)
    value_grad = own_rows[:, group:].astype(jnp.bfloat16)
    query_grad = (query_acc * score_scale).reshape(row_count, group).astype(jnp.bfloat16)
    kernel_total = kernel_sum
    kernel_grad = kernel_total / lax.axis_size("dp")
    early = lax.all_to_all(
        jnp.stack([out, frame_grad]).reshape(2, sub_count, rows, 1, group), "sb", 1, 3, tiled=True
    ).reshape(2, rows, channels)
    late = lax.all_to_all(
        jnp.stack([query_grad, key_grad, value_grad]).reshape(3, sub_count, rows, 1, group),
        "sb",
        1,
        3,
        tiled=True,
    ).reshape(3, rows, channels)
    return (early[0], late[0], late[1], late[2], early[1], kernel_grad)


def solution(mesh):
    seq_count = mesh.shape["seq"]
    split_mesh = Mesh(
        mesh.devices.reshape(mesh.shape["dp"], seq_count // GROUPS, GROUPS),
        ("dp", "sa", "sb"),
    )
    rows_spec = P(("dp", "sa", "sb"), None)
    placed = (rows_spec, rows_spec, rows_spec, rows_spec, rows_spec, P("dp"), P())
    return jax.shard_map(
        per_device,
        mesh=split_mesh,
        in_specs=placed,
        out_specs=(rows_spec, rows_spec, rows_spec, rows_spec, rows_spec, P()),
        check_vma=False,
    )
```

```python
import jax
import jax.numpy as jnp
from jax import lax
from jax.sharding import Mesh
from jax.sharding import PartitionSpec as P

HEAD_DIM = 64
KERNEL = 32
GROUPS = 4


def shifted(x, axis, by):
    count = lax.axis_size(axis)
    pairs = [(i, i + by) for i in range(count) if 0 <= i + by < count]
    return lax.ppermute(x, axis, pairs)


def radix_sum(x, axis):
    count = lax.axis_size(axis)
    position = lax.axis_index(axis)
    received = [x] + [
        lax.ppermute(x, axis, [(i, (i + s) % count) for i in range(count)])
        for s in range(1, count)
    ]
    ordered = jnp.stack(received)[(position - jnp.arange(count)) % count]
    total = ordered[0]
    for j in range(1, count):
        total = total + ordered[j]
    return total


def xor_step(x, axis, step):
    count = lax.axis_size(axis)
    return x + lax.ppermute(x, axis, [(i, i ^ step) for i in range(count)])


def to_blocks(x, rows, sub_count, group):
    return lax.all_to_all(x.reshape(rows, sub_count, group), "sb", 1, 0, tiled=True).reshape(
        rows * sub_count, group
    )


def to_rows(y, rows, sub_count, group):
    return lax.all_to_all(y.reshape(sub_count, rows, 1, group), "sb", 0, 2, tiled=True).reshape(
        rows, sub_count * group
    )


def per_device(queries, keys, values, frames, upstream, lengths, conv_kernel):
    rows = queries.shape[0]
    channels = queries.shape[1]
    sub_count = lax.axis_size("sb")
    block_count_a = lax.axis_size("sa")
    group = channels // sub_count
    head_count = group // HEAD_DIM
    row_count = rows * sub_count
    span = row_count * block_count_a
    block_index = lax.axis_index("sa")
    group_index = lax.axis_index("sb")
    first_row = block_index * row_count
    length = lengths[0]
    score_scale = HEAD_DIM ** (-0.5)

    keys_b = to_blocks(keys, rows, sub_count, group)
    rest = lax.all_to_all(
        jnp.stack([queries, values, frames, upstream]).reshape(4, rows, sub_count, group),
        "sb",
        2,
        1,
        tiled=True,
    ).reshape(4, row_count, group)
    queries_b = rest[0]
    values_b = rest[1]
    frames_b = rest[2]
    upstream_b = rest[3]
    shifts = [[(i, (i + s) % block_count_a) for i in range(block_count_a)] for s in range(1, block_count_a)]
    key_recv = [lax.ppermute(keys_b, "sa", pairs) for pairs in shifts]
    key_recv_tied, values_tied = lax.optimization_barrier((key_recv, values_b))
    value_recv = [lax.ppermute(values_tied, "sa", pairs) for pairs in shifts]
    key_flat = [keys_b] + list(key_recv_tied)
    value_flat = [values_b] + value_recv
    part_blocks = [(block_index - s) % block_count_a for s in range(block_count_a)]
    key_parts = [part.reshape(row_count, head_count, HEAD_DIM) for part in key_flat]
    value_parts = [part.reshape(row_count, head_count, HEAD_DIM) for part in value_flat]
    part_starts = [blk * row_count for blk in part_blocks]
    query_heads = queries_b.reshape(row_count, head_count, HEAD_DIM)

    def block_scores(key_part, block_start):
        scores = (
            jnp.einsum("thd,khd->htk", query_heads, key_part, preferred_element_type=jnp.float32)
            * score_scale
        )
        key_live = block_start + jnp.arange(key_part.shape[0], dtype=jnp.int32) < length
        return jnp.where(key_live[None, None, :], scores, -jnp.inf)

    running_top = jnp.full((head_count, row_count), -1e30, jnp.float32)
    total_sum = jnp.zeros((head_count, row_count), jnp.float32)
    for s in range(block_count_a):
        scores = block_scores(key_parts[s], part_starts[s])
        higher = jnp.maximum(running_top, jnp.max(scores, axis=2))
        total_sum = total_sum * jnp.exp(running_top - higher) + jnp.sum(
            jnp.exp(scores - higher[:, :, None]), axis=2
        )
        running_top = higher
    log_total = running_top + jnp.log(total_sum)

    attend_acc = jnp.zeros((row_count, head_count, HEAD_DIM), jnp.float32)
    for s in range(block_count_a):
        prob_bf = jnp.exp(block_scores(key_parts[s], part_starts[s]) - log_total[:, :, None]).astype(
            jnp.bfloat16
        )
        attend_acc = attend_acc + jnp.einsum(
            "htk,khd->thd", prob_bf, value_parts[s], preferred_element_type=jnp.float32
        )
    attended = attend_acc.reshape(row_count, group).astype(jnp.bfloat16)
    frame_live = (first_row + jnp.arange(row_count, dtype=jnp.int32) < length)[:, None]
    hidden = (frames_b.astype(jnp.float32) + attended.astype(jnp.float32)).astype(jnp.bfloat16)
    masked = jnp.where(frame_live, hidden, jnp.zeros_like(hidden))
    past_rows = shifted(masked[row_count - (KERNEL - 1) :], "sa", 1)
    extended = jnp.concatenate([past_rows, masked], axis=0).astype(jnp.float32)
    weights = lax.dynamic_slice_in_dim(conv_kernel, group_index * group, group, axis=1).astype(
        jnp.float32
    )
    conv_out = jnp.zeros((row_count, group), jnp.float32)
    for tap_index in range(KERNEL):
        conv_out = (
            conv_out
            + weights[tap_index]
            * extended[KERNEL - 1 - tap_index : KERNEL - 1 - tap_index + row_count]
        )
    sig_conv = jax.nn.sigmoid(conv_out)
    out = (hidden.astype(jnp.float32) + conv_out * sig_conv).astype(jnp.bfloat16)
    loss_grad = jnp.where(frame_live, upstream_b.astype(jnp.float32), 0.0)
    conv_grad = (loss_grad * sig_conv * (1.0 + conv_out * (1.0 - sig_conv))).astype(jnp.bfloat16)
    conv_float = conv_grad.astype(jnp.float32)
    kernel_part = jnp.stack(
        [
            jnp.sum(
                conv_float * extended[KERNEL - 1 - tap_index : KERNEL - 1 - tap_index + row_count],
                axis=0,
            )
            for tap_index in range(KERNEL)
        ]
    )
    future_rows = shifted(conv_grad[: KERNEL - 1], "sa", -1)
    ahead_rows = jnp.concatenate([conv_grad, future_rows], axis=0).astype(jnp.float32)
    back_conv = jnp.zeros((row_count, group), jnp.float32)
    for tap_index in range(KERNEL):
        back_conv = back_conv + weights[tap_index] * ahead_rows[tap_index : tap_index + row_count]
    frame_grad = (loss_grad + jnp.where(frame_live, back_conv, 0.0)).astype(jnp.bfloat16)
    grad_heads = frame_grad.reshape(row_count, head_count, HEAD_DIM)
    attended_heads = attended.reshape(row_count, head_count, HEAD_DIM)
    delta_rows = jnp.sum(
        grad_heads.astype(jnp.float32) * attended_heads.astype(jnp.float32), axis=2
    ).T

    def score_grads(key_part, value_part, block_start):
        soft_weights = jnp.exp(block_scores(key_part, block_start) - log_total[:, :, None])
        prob_grad = jnp.einsum(
            "thd,khd->htk", grad_heads, value_part, preferred_element_type=jnp.float32
        )
        score_grad = (soft_weights * (prob_grad - delta_rows[:, :, None])).astype(jnp.bfloat16)
        return (soft_weights.astype(jnp.bfloat16), score_grad)

    query_acc = jnp.zeros((row_count, head_count, HEAD_DIM), jnp.float32)
    own_terms = None
    arrived = []
    kernel_high = kernel_part.astype(jnp.bfloat16)
    kernel_low = (kernel_part - kernel_high.astype(jnp.float32)).astype(jnp.bfloat16)
    kernel_slot = jnp.concatenate(
        [kernel_high, kernel_low, jnp.zeros((rows - 2 * KERNEL, group), jnp.bfloat16)], axis=0
    )
    early = lax.all_to_all(
        jnp.concatenate(
            [
                jnp.stack([out, frame_grad]).reshape(2, sub_count, rows, 1, group),
                jnp.broadcast_to(kernel_slot[None, None, :, None, :], (1, sub_count, rows, 1, group)),
            ],
            axis=0,
        ),
        "sb",
        1,
        3,
        tiled=True,
    ).reshape(3, rows, channels)
    kernel_gathered = (
        early[2, :KERNEL].astype(jnp.float32) + early[2, KERNEL : 2 * KERNEL].astype(jnp.float32)
    )
    kernel_rounds = [
        lambda value: xor_step(xor_step(value, "dp", 1), "dp", 2),
        lambda value: xor_step(xor_step(value, "dp", 4), "dp", 8),
        lambda value: radix_sum(value, "sa"),
        lambda value: value,
    ]
    kernel_sum = kernel_gathered
    for step, s in enumerate(list(range(1, block_count_a)) + [0]):
        kernel_sum = kernel_rounds[step](kernel_sum)
        key_part = key_parts[s]
        value_part = value_parts[s]
        if step > 0:
            kernel_sum, key_part, value_part = lax.optimization_barrier(
                (kernel_sum, key_part, value_part)
            )
        prob_bf, score_grad = score_grads(key_part, value_part, part_starts[s])
        query_acc = query_acc + jnp.einsum(
            "htk,khd->thd", score_grad, key_part, preferred_element_type=jnp.float32
        )
        key_term = (
            jnp.einsum("htk,thd->khd", score_grad, query_heads, preferred_element_type=jnp.float32)
            * score_scale
        )
        value_term = jnp.einsum(
            "htk,thd->khd", prob_bf, grad_heads, preferred_element_type=jnp.float32
        )
        grad_terms = jnp.concatenate(
            [key_term.reshape(row_count, group), value_term.reshape(row_count, group)], axis=1
        ).astype(jnp.bfloat16)
        if s == 0:
            own_terms = grad_terms
        else:
            arrived.append(
                lax.ppermute(
                    grad_terms,
                    "sa",
                    [(i, (i - s) % block_count_a) for i in range(block_count_a)],
                )
            )
    own_rows = own_terms.astype(jnp.float32)
    for part in arrived:
        own_rows = own_rows + part.astype(jnp.float32)
    key_grad = own_rows[:, :group].astype(jnp.bfloat16)
    value_grad = own_rows[:, group:].astype(jnp.bfloat16)
    query_grad = (query_acc * score_scale).reshape(row_count, group).astype(jnp.bfloat16)
    kernel_total = kernel_sum
    kernel_grad = kernel_total / lax.axis_size("dp")
    late = lax.all_to_all(
        jnp.stack([query_grad, key_grad, value_grad]).reshape(3, sub_count, rows, 1, group),
        "sb",
        1,
        3,
        tiled=True,
    ).reshape(3, rows, channels)
    return (early[0], late[0], late[1], late[2], early[1], kernel_grad)


def solution(mesh):
    seq_count = mesh.shape["seq"]
    split_mesh = Mesh(
        mesh.devices.reshape(mesh.shape["dp"], seq_count // GROUPS, GROUPS),
        ("dp", "sa", "sb"),
    )
    rows_spec = P(("dp", "sa", "sb"), None)
    placed = (rows_spec, rows_spec, rows_spec, rows_spec, rows_spec, P("dp"), P())
    return jax.shard_map(
        per_device,
        mesh=split_mesh,
        in_specs=placed,
        out_specs=(rows_spec, rows_spec, rows_spec, rows_spec, rows_spec, P()),
        check_vma=False,
    )
```

```python
import jax
import jax.numpy as jnp
from jax import lax
from jax.sharding import Mesh
from jax.sharding import PartitionSpec as P

HEAD_DIM = 64
KERNEL = 32
GROUPS = 4


def shifted(x, axis, by):
    count = lax.axis_size(axis)
    pairs = [(i, i + by) for i in range(count) if 0 <= i + by < count]
    return lax.ppermute(x, axis, pairs)


def radix_sum(x, axis):
    count = lax.axis_size(axis)
    position = lax.axis_index(axis)
    received = [x] + [
        lax.ppermute(x, axis, [(i, (i + s) % count) for i in range(count)])
        for s in range(1, count)
    ]
    ordered = jnp.stack(received)[(position - jnp.arange(count)) % count]
    total = ordered[0]
    for j in range(1, count):
        total = total + ordered[j]
    return total


def xor_step(x, axis, step):
    count = lax.axis_size(axis)
    return x + lax.ppermute(x, axis, [(i, i ^ step) for i in range(count)])


def to_blocks(x, rows, sub_count, group):
    return lax.all_to_all(x.reshape(rows, sub_count, group), "sb", 1, 0, tiled=True).reshape(
        rows * sub_count, group
    )


def to_rows(y, rows, sub_count, group):
    return lax.all_to_all(y.reshape(sub_count, rows, 1, group), "sb", 0, 2, tiled=True).reshape(
        rows, sub_count * group
    )


def per_device(queries, keys, values, frames, upstream, lengths, conv_kernel):
    rows = queries.shape[0]
    channels = queries.shape[1]
    sub_count = lax.axis_size("sb")
    block_count_a = lax.axis_size("sa")
    group = channels // sub_count
    head_count = group // HEAD_DIM
    row_count = rows * sub_count
    span = row_count * block_count_a
    block_index = lax.axis_index("sa")
    group_index = lax.axis_index("sb")
    row_positions = (
        (jnp.arange(sub_count, dtype=jnp.int32)[:, None] * block_count_a + block_index) * rows
        + jnp.arange(rows, dtype=jnp.int32)[None, :]
    ).reshape(row_count)
    length = lengths[0]
    score_scale = HEAD_DIM ** (-0.5)

    keys_b = to_blocks(keys, rows, sub_count, group)
    rest = lax.all_to_all(
        jnp.stack([queries, values, frames, upstream]).reshape(4, rows, sub_count, group),
        "sb",
        2,
        1,
        tiled=True,
    ).reshape(4, row_count, group)
    queries_b = rest[0]
    values_b = rest[1]
    frames_b = rest[2]
    upstream_b = rest[3]
    shifts = [[(i, (i + s) % block_count_a) for i in range(block_count_a)] for s in range(1, block_count_a)]
    key_recv = [lax.ppermute(keys_b, "sa", pairs) for pairs in shifts]
    key_recv_tied, values_tied = lax.optimization_barrier((key_recv, values_b))
    value_recv = [lax.ppermute(values_tied, "sa", pairs) for pairs in shifts]
    key_flat = [keys_b] + list(key_recv_tied)
    value_flat = [values_b] + value_recv
    part_blocks = [(block_index - s) % block_count_a for s in range(block_count_a)]
    key_parts = [part.reshape(row_count, head_count, HEAD_DIM) for part in key_flat]
    value_parts = [part.reshape(row_count, head_count, HEAD_DIM) for part in value_flat]
    part_positions = [
        (
            (jnp.arange(sub_count, dtype=jnp.int32)[:, None] * block_count_a + blk) * rows
            + jnp.arange(rows, dtype=jnp.int32)[None, :]
        ).reshape(row_count)
        for blk in part_blocks
    ]
    query_heads = queries_b.reshape(row_count, head_count, HEAD_DIM)

    def block_scores(key_part, key_positions):
        scores = (
            jnp.einsum("thd,khd->htk", query_heads, key_part, preferred_element_type=jnp.float32)
            * score_scale
        )
        key_live = key_positions < length
        return jnp.where(key_live[None, None, :], scores, -jnp.inf)

    running_top = jnp.full((head_count, row_count), -1e30, jnp.float32)
    total_sum = jnp.zeros((head_count, row_count), jnp.float32)
    for s in range(block_count_a):
        scores = block_scores(key_parts[s], part_positions[s])
        higher = jnp.maximum(running_top, jnp.max(scores, axis=2))
        total_sum = total_sum * jnp.exp(running_top - higher) + jnp.sum(
            jnp.exp(scores - higher[:, :, None]), axis=2
        )
        running_top = higher
    log_total = running_top + jnp.log(total_sum)

    attend_acc = jnp.zeros((row_count, head_count, HEAD_DIM), jnp.float32)
    for s in range(block_count_a):
        prob_bf = jnp.exp(block_scores(key_parts[s], part_positions[s]) - log_total[:, :, None]).astype(
            jnp.bfloat16
        )
        attend_acc = attend_acc + jnp.einsum(
            "htk,khd->thd", prob_bf, value_parts[s], preferred_element_type=jnp.float32
        )
    attended = attend_acc.reshape(row_count, group).astype(jnp.bfloat16)
    frame_live = (row_positions < length)[:, None]
    hidden = (frames_b.astype(jnp.float32) + attended.astype(jnp.float32)).astype(jnp.bfloat16)
    masked = jnp.where(frame_live, hidden, jnp.zeros_like(hidden))
    masked_subs = masked.reshape(sub_count, rows, group)
    past_recv = lax.ppermute(
        masked_subs[:, rows - (KERNEL - 1) :],
        "sa",
        [(i, (i + 1) % block_count_a) for i in range(block_count_a)],
    )
    past_wrapped = jnp.concatenate([jnp.zeros_like(past_recv[:1]), past_recv[:-1]], axis=0)
    past_rows = jnp.where(block_index == 0, past_wrapped, past_recv)
    extended = jnp.concatenate([past_rows, masked_subs], axis=1).astype(jnp.float32)
    weights = lax.dynamic_slice_in_dim(conv_kernel, group_index * group, group, axis=1).astype(
        jnp.float32
    )
    conv_out = jnp.zeros((sub_count, rows, group), jnp.float32)
    for tap_index in range(KERNEL):
        conv_out = (
            conv_out
            + weights[tap_index]
            * extended[:, KERNEL - 1 - tap_index : KERNEL - 1 - tap_index + rows]
        )
    conv_out = conv_out.reshape(row_count, group)
    sig_conv = jax.nn.sigmoid(conv_out)
    out = (hidden.astype(jnp.float32) + conv_out * sig_conv).astype(jnp.bfloat16)
    loss_grad = jnp.where(frame_live, upstream_b.astype(jnp.float32), 0.0)
    conv_grad = (loss_grad * sig_conv * (1.0 + conv_out * (1.0 - sig_conv))).astype(jnp.bfloat16)
    conv_float = conv_grad.astype(jnp.float32).reshape(sub_count, rows, group)
    kernel_part = jnp.stack(
        [
            jnp.sum(
                conv_float * extended[:, KERNEL - 1 - tap_index : KERNEL - 1 - tap_index + rows],
                axis=(0, 1),
            )
            for tap_index in range(KERNEL)
        ]
    )
    grad_subs = conv_grad.reshape(sub_count, rows, group)
    future_recv = lax.ppermute(
        grad_subs[:, : KERNEL - 1],
        "sa",
        [(i, (i - 1) % block_count_a) for i in range(block_count_a)],
    )
    future_wrapped = jnp.concatenate([future_recv[1:], jnp.zeros_like(future_recv[:1])], axis=0)
    future_rows = jnp.where(block_index == block_count_a - 1, future_wrapped, future_recv)
    ahead_rows = jnp.concatenate([grad_subs, future_rows], axis=1).astype(jnp.float32)
    back_conv = jnp.zeros((sub_count, rows, group), jnp.float32)
    for tap_index in range(KERNEL):
        back_conv = back_conv + weights[tap_index] * ahead_rows[:, tap_index : tap_index + rows]
    back_conv = back_conv.reshape(row_count, group)
    frame_grad = (loss_grad + jnp.where(frame_live, back_conv, 0.0)).astype(jnp.bfloat16)
    grad_heads = frame_grad.reshape(row_count, head_count, HEAD_DIM)
    attended_heads = attended.reshape(row_count, head_count, HEAD_DIM)
    delta_rows = jnp.sum(
        grad_heads.astype(jnp.float32) * attended_heads.astype(jnp.float32), axis=2
    ).T

    def score_grads(key_part, value_part, key_positions):
        soft_weights = jnp.exp(block_scores(key_part, key_positions) - log_total[:, :, None])
        prob_grad = jnp.einsum(
            "thd,khd->htk", grad_heads, value_part, preferred_element_type=jnp.float32
        )
        score_grad = (soft_weights * (prob_grad - delta_rows[:, :, None])).astype(jnp.bfloat16)
        return (soft_weights.astype(jnp.bfloat16), score_grad)

    query_acc = jnp.zeros((row_count, head_count, HEAD_DIM), jnp.float32)
    own_terms = None
    arrived = []
    kernel_rounds = [
        lambda value: radix_sum(value, "sa"),
        lambda value: xor_step(xor_step(value, "dp", 1), "dp", 2),
        lambda value: xor_step(xor_step(value, "dp", 4), "dp", 8),
        lambda value: radix_sum(
            lax.dynamic_update_slice_in_dim(
                jnp.zeros((KERNEL, channels), jnp.float32), value, group_index * group, axis=1
            ),
            "sb",
        ),
    ]
    kernel_sum = kernel_part
    for step, s in enumerate(list(range(1, block_count_a)) + [0]):
        kernel_sum = kernel_rounds[step](kernel_sum)
        key_part = key_parts[s]
        value_part = value_parts[s]
        if step > 0:
            kernel_sum, key_part, value_part = lax.optimization_barrier(
                (kernel_sum, key_part, value_part)
            )
        prob_bf, score_grad = score_grads(key_part, value_part, part_positions[s])
        query_acc = query_acc + jnp.einsum(
            "htk,khd->thd", score_grad, key_part, preferred_element_type=jnp.float32
        )
        key_term = (
            jnp.einsum("htk,thd->khd", score_grad, query_heads, preferred_element_type=jnp.float32)
            * score_scale
        )
        value_term = jnp.einsum(
            "htk,thd->khd", prob_bf, grad_heads, preferred_element_type=jnp.float32
        )
        grad_terms = jnp.concatenate(
            [key_term.reshape(row_count, group), value_term.reshape(row_count, group)], axis=1
        ).astype(jnp.bfloat16)
        if s == 0:
            own_terms = grad_terms
        else:
            arrived.append(
                lax.ppermute(
                    grad_terms,
                    "sa",
                    [(i, (i - s) % block_count_a) for i in range(block_count_a)],
                )
            )
    own_rows = own_terms.astype(jnp.float32)
    for part in arrived:
        own_rows = own_rows + part.astype(jnp.float32)
    key_grad = own_rows[:, :group].astype(jnp.bfloat16)
    value_grad = own_rows[:, group:].astype(jnp.bfloat16)
    query_grad = (query_acc * score_scale).reshape(row_count, group).astype(jnp.bfloat16)
    kernel_total = kernel_sum
    kernel_grad = kernel_total / lax.axis_size("dp")
    early = lax.all_to_all(
        jnp.stack([out, frame_grad]).reshape(2, sub_count, rows, 1, group), "sb", 1, 3, tiled=True
    ).reshape(2, rows, channels)
    late = lax.all_to_all(
        jnp.stack([query_grad, key_grad, value_grad]).reshape(3, sub_count, rows, 1, group),
        "sb",
        1,
        3,
        tiled=True,
    ).reshape(3, rows, channels)
    return (early[0], late[0], late[1], late[2], early[1], kernel_grad)


def solution(mesh):
    seq_count = mesh.shape["seq"]
    split_mesh = Mesh(
        mesh.devices.reshape(mesh.shape["dp"], GROUPS, seq_count // GROUPS),
        ("dp", "sb", "sa"),
    )
    rows_spec = P(("dp", "sb", "sa"), None)
    placed = (rows_spec, rows_spec, rows_spec, rows_spec, rows_spec, P("dp"), P())
    return jax.shard_map(
        per_device,
        mesh=split_mesh,
        in_specs=placed,
        out_specs=(rows_spec, rows_spec, rows_spec, rows_spec, rows_spec, P()),
        check_vma=False,
    )
```

```python
import jax
import jax.numpy as jnp
from jax import lax
from jax.sharding import Mesh
from jax.sharding import PartitionSpec as P

HEAD_DIM = 64
KERNEL = 32
GROUPS = 4


def shifted(x, axis, by):
    count = lax.axis_size(axis)
    pairs = [(i, i + by) for i in range(count) if 0 <= i + by < count]
    return lax.ppermute(x, axis, pairs)


def radix_sum(x, axis):
    count = lax.axis_size(axis)
    position = lax.axis_index(axis)
    received = [x] + [
        lax.ppermute(x, axis, [(i, (i + s) % count) for i in range(count)])
        for s in range(1, count)
    ]
    ordered = jnp.stack(received)[(position - jnp.arange(count)) % count]
    total = ordered[0]
    for j in range(1, count):
        total = total + ordered[j]
    return total


def xor_step(x, axis, step):
    count = lax.axis_size(axis)
    return x + lax.ppermute(x, axis, [(i, i ^ step) for i in range(count)])


def to_blocks(x, rows, sub_count, group):
    return lax.all_to_all(x.reshape(rows, sub_count, group), "sb", 1, 0, tiled=True).reshape(
        rows * sub_count, group
    )


def to_rows(y, rows, sub_count, group):
    return lax.all_to_all(y.reshape(sub_count, rows, 1, group), "sb", 0, 2, tiled=True).reshape(
        rows, sub_count * group
    )


def per_device(queries, keys, values, frames, upstream, lengths, conv_kernel):
    rows = queries.shape[0]
    channels = queries.shape[1]
    sub_count = lax.axis_size("sb")
    block_count_a = lax.axis_size("sa")
    group = channels // sub_count
    head_count = group // HEAD_DIM
    row_count = rows * sub_count
    span = row_count * block_count_a
    block_index = lax.axis_index("sa")
    group_index = lax.axis_index("sb")
    first_row = block_index * row_count
    length = lengths[0]
    score_scale = HEAD_DIM ** (-0.5)

    rest = lax.all_to_all(
        jnp.stack([queries, values, frames, upstream]).reshape(4, rows, sub_count, group),
        "sb",
        2,
        1,
        tiled=True,
    ).reshape(4, row_count, group)
    queries_b = rest[0]
    values_b = rest[1]
    frames_b = rest[2]
    upstream_b = rest[3]
    shifts = [[(i, (i + s) % block_count_a) for i in range(block_count_a)] for s in range(1, block_count_a)]
    key_rows = [keys] + [lax.ppermute(keys, "sa", pairs) for pairs in shifts]
    key_stack = lax.all_to_all(
        jnp.stack(key_rows).reshape(block_count_a, rows, sub_count, group), "sb", 2, 1, tiled=True
    ).reshape(block_count_a, row_count, group)
    keys_b = key_stack[0]
    key_recv = [key_stack[s] for s in range(1, block_count_a)]
    key_recv_tied, values_tied = lax.optimization_barrier((key_recv, values_b))
    value_recv = [lax.ppermute(values_tied, "sa", pairs) for pairs in shifts]
    key_flat = [keys_b] + list(key_recv_tied)
    value_flat = [values_b] + value_recv
    part_blocks = [(block_index - s) % block_count_a for s in range(block_count_a)]
    key_parts = [part.reshape(row_count, head_count, HEAD_DIM) for part in key_flat]
    value_parts = [part.reshape(row_count, head_count, HEAD_DIM) for part in value_flat]
    part_starts = [blk * row_count for blk in part_blocks]
    query_heads = queries_b.reshape(row_count, head_count, HEAD_DIM)

    def block_scores(key_part, block_start):
        scores = (
            jnp.einsum("thd,khd->htk", query_heads, key_part, preferred_element_type=jnp.float32)
            * score_scale
        )
        key_live = block_start + jnp.arange(key_part.shape[0], dtype=jnp.int32) < length
        return jnp.where(key_live[None, None, :], scores, -jnp.inf)

    running_top = jnp.full((head_count, row_count), -1e30, jnp.float32)
    total_sum = jnp.zeros((head_count, row_count), jnp.float32)
    for s in range(block_count_a):
        scores = block_scores(key_parts[s], part_starts[s])
        higher = jnp.maximum(running_top, jnp.max(scores, axis=2))
        total_sum = total_sum * jnp.exp(running_top - higher) + jnp.sum(
            jnp.exp(scores - higher[:, :, None]), axis=2
        )
        running_top = higher
    log_total = running_top + jnp.log(total_sum)

    attend_acc = jnp.zeros((row_count, head_count, HEAD_DIM), jnp.float32)
    for s in range(block_count_a):
        prob_bf = jnp.exp(block_scores(key_parts[s], part_starts[s]) - log_total[:, :, None]).astype(
            jnp.bfloat16
        )
        attend_acc = attend_acc + jnp.einsum(
            "htk,khd->thd", prob_bf, value_parts[s], preferred_element_type=jnp.float32
        )
    attended = attend_acc.reshape(row_count, group).astype(jnp.bfloat16)
    frame_live = (first_row + jnp.arange(row_count, dtype=jnp.int32) < length)[:, None]
    hidden = (frames_b.astype(jnp.float32) + attended.astype(jnp.float32)).astype(jnp.bfloat16)
    masked = jnp.where(frame_live, hidden, jnp.zeros_like(hidden))
    past_rows = shifted(masked[row_count - (KERNEL - 1) :], "sa", 1)
    extended = jnp.concatenate([past_rows, masked], axis=0).astype(jnp.float32)
    weights = lax.dynamic_slice_in_dim(conv_kernel, group_index * group, group, axis=1).astype(
        jnp.float32
    )
    conv_out = jnp.zeros((row_count, group), jnp.float32)
    for tap_index in range(KERNEL):
        conv_out = (
            conv_out
            + weights[tap_index]
            * extended[KERNEL - 1 - tap_index : KERNEL - 1 - tap_index + row_count]
        )
    sig_conv = jax.nn.sigmoid(conv_out)
    out = (hidden.astype(jnp.float32) + conv_out * sig_conv).astype(jnp.bfloat16)
    loss_grad = jnp.where(frame_live, upstream_b.astype(jnp.float32), 0.0)
    conv_grad = (loss_grad * sig_conv * (1.0 + conv_out * (1.0 - sig_conv))).astype(jnp.bfloat16)
    conv_float = conv_grad.astype(jnp.float32)
    kernel_part = jnp.stack(
        [
            jnp.sum(
                conv_float * extended[KERNEL - 1 - tap_index : KERNEL - 1 - tap_index + row_count],
                axis=0,
            )
            for tap_index in range(KERNEL)
        ]
    )
    future_rows = shifted(conv_grad[: KERNEL - 1], "sa", -1)
    ahead_rows = jnp.concatenate([conv_grad, future_rows], axis=0).astype(jnp.float32)
    back_conv = jnp.zeros((row_count, group), jnp.float32)
    for tap_index in range(KERNEL):
        back_conv = back_conv + weights[tap_index] * ahead_rows[tap_index : tap_index + row_count]
    frame_grad = (loss_grad + jnp.where(frame_live, back_conv, 0.0)).astype(jnp.bfloat16)
    grad_heads = frame_grad.reshape(row_count, head_count, HEAD_DIM)
    attended_heads = attended.reshape(row_count, head_count, HEAD_DIM)
    delta_rows = jnp.sum(
        grad_heads.astype(jnp.float32) * attended_heads.astype(jnp.float32), axis=2
    ).T

    def score_grads(key_part, value_part, block_start):
        soft_weights = jnp.exp(block_scores(key_part, block_start) - log_total[:, :, None])
        prob_grad = jnp.einsum(
            "thd,khd->htk", grad_heads, value_part, preferred_element_type=jnp.float32
        )
        score_grad = (soft_weights * (prob_grad - delta_rows[:, :, None])).astype(jnp.bfloat16)
        return (soft_weights.astype(jnp.bfloat16), score_grad)

    query_acc = jnp.zeros((row_count, head_count, HEAD_DIM), jnp.float32)
    own_terms = None
    arrived = []
    kernel_rounds = [
        lambda value: radix_sum(value, "sa"),
        lambda value: xor_step(xor_step(value, "dp", 1), "dp", 2),
        lambda value: xor_step(xor_step(value, "dp", 4), "dp", 8),
        lambda value: radix_sum(
            lax.dynamic_update_slice_in_dim(
                jnp.zeros((KERNEL, channels), jnp.float32), value, group_index * group, axis=1
            ),
            "sb",
        ),
    ]
    kernel_sum = kernel_part
    for step, s in enumerate(list(range(1, block_count_a)) + [0]):
        kernel_sum = kernel_rounds[step](kernel_sum)
        key_part = key_parts[s]
        value_part = value_parts[s]
        if step > 0:
            kernel_sum, key_part, value_part = lax.optimization_barrier(
                (kernel_sum, key_part, value_part)
            )
        prob_bf, score_grad = score_grads(key_part, value_part, part_starts[s])
        query_acc = query_acc + jnp.einsum(
            "htk,khd->thd", score_grad, key_part, preferred_element_type=jnp.float32
        )
        key_term = (
            jnp.einsum("htk,thd->khd", score_grad, query_heads, preferred_element_type=jnp.float32)
            * score_scale
        )
        value_term = jnp.einsum(
            "htk,thd->khd", prob_bf, grad_heads, preferred_element_type=jnp.float32
        )
        grad_terms = jnp.concatenate(
            [key_term.reshape(row_count, group), value_term.reshape(row_count, group)], axis=1
        ).astype(jnp.bfloat16)
        if s == 0:
            own_terms = grad_terms
        else:
            arrived.append(
                lax.ppermute(
                    grad_terms,
                    "sa",
                    [(i, (i - s) % block_count_a) for i in range(block_count_a)],
                )
            )
    own_rows = own_terms.astype(jnp.float32)
    for part in arrived:
        own_rows = own_rows + part.astype(jnp.float32)
    key_grad = own_rows[:, :group].astype(jnp.bfloat16)
    value_grad = own_rows[:, group:].astype(jnp.bfloat16)
    query_grad = (query_acc * score_scale).reshape(row_count, group).astype(jnp.bfloat16)
    kernel_total = kernel_sum
    kernel_grad = kernel_total / lax.axis_size("dp")
    early = lax.all_to_all(
        jnp.stack([out, frame_grad]).reshape(2, sub_count, rows, 1, group), "sb", 1, 3, tiled=True
    ).reshape(2, rows, channels)
    late = lax.all_to_all(
        jnp.stack([query_grad, key_grad, value_grad]).reshape(3, sub_count, rows, 1, group),
        "sb",
        1,
        3,
        tiled=True,
    ).reshape(3, rows, channels)
    return (early[0], late[0], late[1], late[2], early[1], kernel_grad)


def solution(mesh):
    seq_count = mesh.shape["seq"]
    split_mesh = Mesh(
        mesh.devices.reshape(mesh.shape["dp"], seq_count // GROUPS, GROUPS),
        ("dp", "sa", "sb"),
    )
    rows_spec = P(("dp", "sa", "sb"), None)
    placed = (rows_spec, rows_spec, rows_spec, rows_spec, rows_spec, P("dp"), P())
    return jax.shard_map(
        per_device,
        mesh=split_mesh,
        in_specs=placed,
        out_specs=(rows_spec, rows_spec, rows_spec, rows_spec, rows_spec, P()),
        check_vma=False,
    )
```

```python
import jax
import jax.numpy as jnp
from jax import lax
from jax.sharding import Mesh
from jax.sharding import PartitionSpec as P

HEAD_DIM = 64
KERNEL = 32
GROUPS = 4


def shifted(x, axis, by):
    count = lax.axis_size(axis)
    pairs = [(i, i + by) for i in range(count) if 0 <= i + by < count]
    return lax.ppermute(x, axis, pairs)


def radix_sum(x, axis):
    count = lax.axis_size(axis)
    position = lax.axis_index(axis)
    received = [x] + [
        lax.ppermute(x, axis, [(i, (i + s) % count) for i in range(count)])
        for s in range(1, count)
    ]
    ordered = jnp.stack(received)[(position - jnp.arange(count)) % count]
    total = ordered[0]
    for j in range(1, count):
        total = total + ordered[j]
    return total


def xor_step(x, axis, step):
    count = lax.axis_size(axis)
    return x + lax.ppermute(x, axis, [(i, i ^ step) for i in range(count)])


def to_blocks(x, rows, sub_count, group):
    return lax.all_to_all(x.reshape(rows, sub_count, group), "sb", 1, 0, tiled=True).reshape(
        rows * sub_count, group
    )


def to_rows(y, rows, sub_count, group):
    return lax.all_to_all(y.reshape(sub_count, rows, 1, group), "sb", 0, 2, tiled=True).reshape(
        rows, sub_count * group
    )


def per_device(queries, keys, values, frames, upstream, lengths, conv_kernel):
    rows = queries.shape[0]
    channels = queries.shape[1]
    sub_count = lax.axis_size("sb")
    block_count_a = lax.axis_size("sa")
    group = channels // sub_count
    head_count = group // HEAD_DIM
    row_count = rows * sub_count
    span = row_count * block_count_a
    block_index = lax.axis_index("sa")
    group_index = lax.axis_index("sb")
    first_row = block_index * row_count
    length = lengths[0]
    score_scale = HEAD_DIM ** (-0.5)

    keys_b = to_blocks(keys, rows, sub_count, group)
    rest = lax.all_to_all(
        jnp.stack([queries, values, frames, upstream]).reshape(4, rows, sub_count, group),
        "sb",
        2,
        1,
        tiled=True,
    ).reshape(4, row_count, group)
    queries_b = rest[0]
    values_b = rest[1]
    frames_b = rest[2]
    upstream_b = rest[3]
    shifts = [[(i, (i + s) % block_count_a) for i in range(block_count_a)] for s in range(1, block_count_a)]
    key_recv = [lax.ppermute(keys_b, "sa", pairs) for pairs in shifts]
    key_recv_tied, values_tied = lax.optimization_barrier((key_recv, values_b))
    value_recv = [lax.ppermute(values_tied, "sa", pairs) for pairs in shifts]
    key_flat = [keys_b] + list(key_recv_tied)
    value_flat = [values_b] + value_recv
    part_blocks = [(block_index - s) % block_count_a for s in range(block_count_a)]
    key_parts = [part.reshape(row_count, head_count, HEAD_DIM) for part in key_flat]
    value_parts = [part.reshape(row_count, head_count, HEAD_DIM) for part in value_flat]
    part_starts = [blk * row_count for blk in part_blocks]
    query_heads = queries_b.reshape(row_count, head_count, HEAD_DIM)

    def block_scores(key_part, block_start):
        scores = (
            jnp.einsum("thd,khd->htk", query_heads, key_part, preferred_element_type=jnp.float32)
            * score_scale
        )
        key_live = block_start + jnp.arange(key_part.shape[0], dtype=jnp.int32) < length
        return jnp.where(key_live[None, None, :], scores, -jnp.inf)

    running_top = jnp.full((head_count, row_count), -1e30, jnp.float32)
    total_sum = jnp.zeros((head_count, row_count), jnp.float32)
    for s in [0, 1, 3, 2][:block_count_a]:
        scores = block_scores(key_parts[s], part_starts[s])
        higher = jnp.maximum(running_top, jnp.max(scores, axis=2))
        total_sum = total_sum * jnp.exp(running_top - higher) + jnp.sum(
            jnp.exp(scores - higher[:, :, None]), axis=2
        )
        running_top = higher
    log_total = running_top + jnp.log(total_sum)

    attend_acc = jnp.zeros((row_count, head_count, HEAD_DIM), jnp.float32)
    for s in range(block_count_a):
        prob_bf = jnp.exp(block_scores(key_parts[s], part_starts[s]) - log_total[:, :, None]).astype(
            jnp.bfloat16
        )
        attend_acc = attend_acc + jnp.einsum(
            "htk,khd->thd", prob_bf, value_parts[s], preferred_element_type=jnp.float32
        )
    attended = attend_acc.reshape(row_count, group).astype(jnp.bfloat16)
    frame_live = (first_row + jnp.arange(row_count, dtype=jnp.int32) < length)[:, None]
    hidden = (frames_b.astype(jnp.float32) + attended.astype(jnp.float32)).astype(jnp.bfloat16)
    masked = jnp.where(frame_live, hidden, jnp.zeros_like(hidden))
    past_rows = shifted(masked[row_count - (KERNEL - 1) :], "sa", 1)
    extended = jnp.concatenate([past_rows, masked], axis=0).astype(jnp.float32)
    weights = lax.dynamic_slice_in_dim(conv_kernel, group_index * group, group, axis=1).astype(
        jnp.float32
    )
    conv_out = jnp.zeros((row_count, group), jnp.float32)
    for tap_index in range(KERNEL):
        conv_out = (
            conv_out
            + weights[tap_index]
            * extended[KERNEL - 1 - tap_index : KERNEL - 1 - tap_index + row_count]
        )
    sig_conv = jax.nn.sigmoid(conv_out)
    out = (hidden.astype(jnp.float32) + conv_out * sig_conv).astype(jnp.bfloat16)
    loss_grad = jnp.where(frame_live, upstream_b.astype(jnp.float32), 0.0)
    conv_grad = (loss_grad * sig_conv * (1.0 + conv_out * (1.0 - sig_conv))).astype(jnp.bfloat16)
    conv_float = conv_grad.astype(jnp.float32)
    kernel_part = jnp.stack(
        [
            jnp.sum(
                conv_float * extended[KERNEL - 1 - tap_index : KERNEL - 1 - tap_index + row_count],
                axis=0,
            )
            for tap_index in range(KERNEL)
        ]
    )
    future_rows = shifted(conv_grad[: KERNEL - 1], "sa", -1)
    ahead_rows = jnp.concatenate([conv_grad, future_rows], axis=0).astype(jnp.float32)
    back_conv = jnp.zeros((row_count, group), jnp.float32)
    for tap_index in range(KERNEL):
        back_conv = back_conv + weights[tap_index] * ahead_rows[tap_index : tap_index + row_count]
    frame_grad = (loss_grad + jnp.where(frame_live, back_conv, 0.0)).astype(jnp.bfloat16)
    grad_heads = frame_grad.reshape(row_count, head_count, HEAD_DIM)
    attended_heads = attended.reshape(row_count, head_count, HEAD_DIM)
    delta_rows = jnp.sum(
        grad_heads.astype(jnp.float32) * attended_heads.astype(jnp.float32), axis=2
    ).T

    def score_grads(key_part, value_part, block_start):
        soft_weights = jnp.exp(block_scores(key_part, block_start) - log_total[:, :, None])
        prob_grad = jnp.einsum(
            "thd,khd->htk", grad_heads, value_part, preferred_element_type=jnp.float32
        )
        score_grad = (soft_weights * (prob_grad - delta_rows[:, :, None])).astype(jnp.bfloat16)
        return (soft_weights.astype(jnp.bfloat16), score_grad)

    query_acc = jnp.zeros((row_count, head_count, HEAD_DIM), jnp.float32)
    own_terms = None
    arrived = []
    kernel_rounds = [
        lambda value: radix_sum(value, "sa"),
        lambda value: xor_step(xor_step(value, "dp", 1), "dp", 2),
        lambda value: xor_step(xor_step(value, "dp", 4), "dp", 8),
        lambda value: radix_sum(
            lax.dynamic_update_slice_in_dim(
                jnp.zeros((KERNEL, channels), jnp.float32), value, group_index * group, axis=1
            ),
            "sb",
        ),
    ]
    kernel_sum = kernel_part
    for step, s in enumerate(list(range(1, block_count_a)) + [0]):
        kernel_sum = kernel_rounds[step](kernel_sum)
        key_part = key_parts[s]
        value_part = value_parts[s]
        if step > 0:
            kernel_sum, key_part, value_part = lax.optimization_barrier(
                (kernel_sum, key_part, value_part)
            )
        prob_bf, score_grad = score_grads(key_part, value_part, part_starts[s])
        query_acc = query_acc + jnp.einsum(
            "htk,khd->thd", score_grad, key_part, preferred_element_type=jnp.float32
        )
        key_term = (
            jnp.einsum("htk,thd->khd", score_grad, query_heads, preferred_element_type=jnp.float32)
            * score_scale
        )
        value_term = jnp.einsum(
            "htk,thd->khd", prob_bf, grad_heads, preferred_element_type=jnp.float32
        )
        grad_terms = jnp.concatenate(
            [key_term.reshape(row_count, group), value_term.reshape(row_count, group)], axis=1
        ).astype(jnp.bfloat16)
        if s == 0:
            own_terms = grad_terms
        else:
            arrived.append(
                lax.ppermute(
                    grad_terms,
                    "sa",
                    [(i, (i - s) % block_count_a) for i in range(block_count_a)],
                )
            )
    own_rows = own_terms.astype(jnp.float32)
    for part in arrived:
        own_rows = own_rows + part.astype(jnp.float32)
    key_grad = own_rows[:, :group].astype(jnp.bfloat16)
    value_grad = own_rows[:, group:].astype(jnp.bfloat16)
    query_grad = (query_acc * score_scale).reshape(row_count, group).astype(jnp.bfloat16)
    kernel_total = kernel_sum
    kernel_grad = kernel_total / lax.axis_size("dp")
    early = lax.all_to_all(
        jnp.stack([out, frame_grad]).reshape(2, sub_count, rows, 1, group), "sb", 1, 3, tiled=True
    ).reshape(2, rows, channels)
    late = lax.all_to_all(
        jnp.stack([query_grad, key_grad, value_grad]).reshape(3, sub_count, rows, 1, group),
        "sb",
        1,
        3,
        tiled=True,
    ).reshape(3, rows, channels)
    return (early[0], late[0], late[1], late[2], early[1], kernel_grad)


def solution(mesh):
    seq_count = mesh.shape["seq"]
    split_mesh = Mesh(
        mesh.devices.reshape(mesh.shape["dp"], seq_count // GROUPS, GROUPS),
        ("dp", "sa", "sb"),
    )
    rows_spec = P(("dp", "sa", "sb"), None)
    placed = (rows_spec, rows_spec, rows_spec, rows_spec, rows_spec, P("dp"), P())
    return jax.shard_map(
        per_device,
        mesh=split_mesh,
        in_specs=placed,
        out_specs=(rows_spec, rows_spec, rows_spec, rows_spec, rows_spec, P()),
        check_vma=False,
    )
```

```python
import jax
import jax.numpy as jnp
from jax import lax
from jax.sharding import Mesh
from jax.sharding import PartitionSpec as P

HEAD_DIM = 64
KERNEL = 32
GROUPS = 4


def shifted(x, axis, by):
    count = lax.axis_size(axis)
    pairs = [(i, i + by) for i in range(count) if 0 <= i + by < count]
    return lax.ppermute(x, axis, pairs)


def radix_sum(x, axis):
    count = lax.axis_size(axis)
    position = lax.axis_index(axis)
    received = [x] + [
        lax.ppermute(x, axis, [(i, (i + s) % count) for i in range(count)])
        for s in range(1, count)
    ]
    ordered = jnp.stack(received)[(position - jnp.arange(count)) % count]
    total = ordered[0]
    for j in range(1, count):
        total = total + ordered[j]
    return total


def xor_step(x, axis, step):
    count = lax.axis_size(axis)
    return x + lax.ppermute(x, axis, [(i, i ^ step) for i in range(count)])


def to_blocks(x, rows, sub_count, group):
    return lax.all_to_all(x.reshape(rows, sub_count, group), "sb", 1, 0, tiled=True).reshape(
        rows * sub_count, group
    )


def to_rows(y, rows, sub_count, group):
    return lax.all_to_all(y.reshape(sub_count, rows, 1, group), "sb", 0, 2, tiled=True).reshape(
        rows, sub_count * group
    )


def per_device(queries, keys, values, frames, upstream, lengths, conv_kernel):
    rows = queries.shape[0]
    channels = queries.shape[1]
    sub_count = lax.axis_size("sb")
    block_count_a = lax.axis_size("sa")
    group = channels // sub_count
    head_count = group // HEAD_DIM
    row_count = rows * sub_count
    span = row_count * block_count_a
    block_index = lax.axis_index("sa")
    group_index = lax.axis_index("sb")
    first_row = block_index * row_count
    length = lengths[0]
    score_scale = HEAD_DIM ** (-0.5)

    keys_b = to_blocks(keys, rows, sub_count, group)
    rest = lax.all_to_all(
        jnp.stack([queries, values, frames, upstream]).reshape(4, rows, sub_count, group),
        "sb",
        2,
        1,
        tiled=True,
    ).reshape(4, row_count, group)
    queries_b = rest[0]
    values_b = rest[1]
    frames_b = rest[2]
    upstream_b = rest[3]
    shifts = [[(i, (i + s) % block_count_a) for i in range(block_count_a)] for s in range(1, block_count_a)]
    key_recv = [lax.ppermute(keys_b, "sa", pairs) for pairs in shifts]
    key_recv_tied, values_tied = lax.optimization_barrier((key_recv, values_b))
    value_recv = [lax.ppermute(values_tied, "sa", pairs) for pairs in shifts]
    key_flat = [keys_b] + key_recv
    value_flat = [values_b] + value_recv
    part_blocks = [(block_index - s) % block_count_a for s in range(block_count_a)]
    key_parts = [part.reshape(row_count, head_count, HEAD_DIM) for part in key_flat]
    value_parts = [part.reshape(row_count, head_count, HEAD_DIM) for part in value_flat]
    part_starts = [blk * row_count for blk in part_blocks]
    query_heads = queries_b.reshape(row_count, head_count, HEAD_DIM)

    def block_scores(key_part, block_start):
        scores = (
            jnp.einsum("thd,khd->htk", query_heads, key_part, preferred_element_type=jnp.float32)
            * score_scale
        )
        key_live = block_start + jnp.arange(key_part.shape[0], dtype=jnp.int32) < length
        return jnp.where(key_live[None, None, :], scores, -jnp.inf)

    running_top = jnp.full((head_count, row_count), -1e30, jnp.float32)
    total_sum = jnp.zeros((head_count, row_count), jnp.float32)
    for s in [0, 1, 3, 2][:block_count_a]:
        scores = block_scores(key_parts[s], part_starts[s])
        higher = jnp.maximum(running_top, jnp.max(scores, axis=2))
        total_sum = total_sum * jnp.exp(running_top - higher) + jnp.sum(
            jnp.exp(scores - higher[:, :, None]), axis=2
        )
        running_top = higher
    log_total = running_top + jnp.log(total_sum)

    attend_acc = jnp.zeros((row_count, head_count, HEAD_DIM), jnp.float32)
    for s in range(block_count_a):
        prob_bf = jnp.exp(block_scores(key_parts[s], part_starts[s]) - log_total[:, :, None]).astype(
            jnp.bfloat16
        )
        attend_acc = attend_acc + jnp.einsum(
            "htk,khd->thd", prob_bf, value_parts[s], preferred_element_type=jnp.float32
        )
    attended = attend_acc.reshape(row_count, group).astype(jnp.bfloat16)
    frame_live = (first_row + jnp.arange(row_count, dtype=jnp.int32) < length)[:, None]
    hidden = (frames_b.astype(jnp.float32) + attended.astype(jnp.float32)).astype(jnp.bfloat16)
    masked = jnp.where(frame_live, hidden, jnp.zeros_like(hidden))
    past_rows = shifted(masked[row_count - (KERNEL - 1) :], "sa", 1)
    extended = jnp.concatenate([past_rows, masked], axis=0).astype(jnp.float32)
    weights = lax.dynamic_slice_in_dim(conv_kernel, group_index * group, group, axis=1).astype(
        jnp.float32
    )
    conv_out = jnp.zeros((row_count, group), jnp.float32)
    for tap_index in range(KERNEL):
        conv_out = (
            conv_out
            + weights[tap_index]
            * extended[KERNEL - 1 - tap_index : KERNEL - 1 - tap_index + row_count]
        )
    sig_conv = jax.nn.sigmoid(conv_out)
    out = (hidden.astype(jnp.float32) + conv_out * sig_conv).astype(jnp.bfloat16)
    loss_grad = jnp.where(frame_live, upstream_b.astype(jnp.float32), 0.0)
    conv_grad = (loss_grad * sig_conv * (1.0 + conv_out * (1.0 - sig_conv))).astype(jnp.bfloat16)
    conv_float = conv_grad.astype(jnp.float32)
    kernel_part = jnp.stack(
        [
            jnp.sum(
                conv_float * extended[KERNEL - 1 - tap_index : KERNEL - 1 - tap_index + row_count],
                axis=0,
            )
            for tap_index in range(KERNEL)
        ]
    )
    future_rows = shifted(conv_grad[: KERNEL - 1], "sa", -1)
    ahead_rows = jnp.concatenate([conv_grad, future_rows], axis=0).astype(jnp.float32)
    back_conv = jnp.zeros((row_count, group), jnp.float32)
    for tap_index in range(KERNEL):
        back_conv = back_conv + weights[tap_index] * ahead_rows[tap_index : tap_index + row_count]
    frame_grad = (loss_grad + jnp.where(frame_live, back_conv, 0.0)).astype(jnp.bfloat16)
    grad_heads = frame_grad.reshape(row_count, head_count, HEAD_DIM)
    attended_heads = attended.reshape(row_count, head_count, HEAD_DIM)
    delta_rows = jnp.sum(
        grad_heads.astype(jnp.float32) * attended_heads.astype(jnp.float32), axis=2
    ).T

    def score_grads(key_part, value_part, block_start):
        soft_weights = jnp.exp(block_scores(key_part, block_start) - log_total[:, :, None])
        prob_grad = jnp.einsum(
            "thd,khd->htk", grad_heads, value_part, preferred_element_type=jnp.float32
        )
        score_grad = (soft_weights * (prob_grad - delta_rows[:, :, None])).astype(jnp.bfloat16)
        return (soft_weights.astype(jnp.bfloat16), score_grad)

    query_acc = jnp.zeros((row_count, head_count, HEAD_DIM), jnp.float32)
    own_terms = None
    arrived = []
    kernel_rounds = [
        lambda value: radix_sum(value, "sa"),
        lambda value: xor_step(xor_step(value, "dp", 1), "dp", 2),
        lambda value: xor_step(xor_step(value, "dp", 4), "dp", 8),
        lambda value: radix_sum(
            lax.dynamic_update_slice_in_dim(
                jnp.zeros((KERNEL, channels), jnp.float32), value, group_index * group, axis=1
            ),
            "sb",
        ),
    ]
    kernel_sum = kernel_part
    for step, s in enumerate(list(range(1, block_count_a)) + [0]):
        kernel_sum = kernel_rounds[step](kernel_sum)
        key_part = key_parts[s]
        value_part = value_parts[s]
        if step > 0:
            kernel_sum, key_part, value_part = lax.optimization_barrier(
                (kernel_sum, key_part, value_part)
            )
        prob_bf, score_grad = score_grads(key_part, value_part, part_starts[s])
        query_acc = query_acc + jnp.einsum(
            "htk,khd->thd", score_grad, key_part, preferred_element_type=jnp.float32
        )
        key_term = (
            jnp.einsum("htk,thd->khd", score_grad, query_heads, preferred_element_type=jnp.float32)
            * score_scale
        )
        value_term = jnp.einsum(
            "htk,thd->khd", prob_bf, grad_heads, preferred_element_type=jnp.float32
        )
        grad_terms = jnp.concatenate(
            [key_term.reshape(row_count, group), value_term.reshape(row_count, group)], axis=1
        ).astype(jnp.bfloat16)
        if s == 0:
            own_terms = grad_terms
        else:
            arrived.append(
                lax.ppermute(
                    grad_terms,
                    "sa",
                    [(i, (i - s) % block_count_a) for i in range(block_count_a)],
                )
            )
    own_rows = own_terms.astype(jnp.float32)
    for part in arrived:
        own_rows = own_rows + part.astype(jnp.float32)
    key_grad = own_rows[:, :group].astype(jnp.bfloat16)
    value_grad = own_rows[:, group:].astype(jnp.bfloat16)
    query_grad = (query_acc * score_scale).reshape(row_count, group).astype(jnp.bfloat16)
    kernel_total = kernel_sum
    kernel_grad = kernel_total / lax.axis_size("dp")
    early = lax.all_to_all(
        jnp.stack([out, frame_grad]).reshape(2, sub_count, rows, 1, group), "sb", 1, 3, tiled=True
    ).reshape(2, rows, channels)
    late = lax.all_to_all(
        jnp.stack([query_grad, key_grad, value_grad]).reshape(3, sub_count, rows, 1, group),
        "sb",
        1,
        3,
        tiled=True,
    ).reshape(3, rows, channels)
    return (early[0], late[0], late[1], late[2], early[1], kernel_grad)


def solution(mesh):
    seq_count = mesh.shape["seq"]
    split_mesh = Mesh(
        mesh.devices.reshape(mesh.shape["dp"], seq_count // GROUPS, GROUPS),
        ("dp", "sa", "sb"),
    )
    rows_spec = P(("dp", "sa", "sb"), None)
    placed = (rows_spec, rows_spec, rows_spec, rows_spec, rows_spec, P("dp"), P())
    return jax.shard_map(
        per_device,
        mesh=split_mesh,
        in_specs=placed,
        out_specs=(rows_spec, rows_spec, rows_spec, rows_spec, rows_spec, P()),
        check_vma=False,
    )
```
